256 devices in a mesh: ctx: 16 (over x, z_hi, core), exp: 16 (over z_lo, y).
Axes of the slice: x: 4, y: 4, z: 8 (z_hi: 2, z_lo: 4; z = z_hi * 4 + z_lo), core: 2. Of those that a mesh axis runs over, the one named last changes fastest.
Arguments:
- queries: bfloat16 [16, 1024, 2560], P('exp', 'ctx'), may hold values from -4.5 to 4.5
- keys: bfloat16 [16, 1024, 512], P('exp', 'ctx'), may hold values from -4.5 to 4.5
- values: bfloat16 [16, 1024, 512], P('exp', 'ctx'), may hold values from -6 to 6
- doc_lengths: int32 [16, 4], P('exp'), may hold values from 1 to 512, 1024 in all within a row
- resid: bfloat16 [16, 1024, 5120], P('exp', 'ctx'), may hold values from -6 to 6
- out_weight: bfloat16 [2560, 5120], P(('ctx', 'exp')), may hold values from -1 to 1
- norm_gain: bfloat16 [5120], replicated, may hold values from 0.099609375 to 1.8984375
- router_weight: bfloat16 [5120, 16], replicated, may hold values from -0.078125 to 0.078125
- expert_ids: int32 [16, 1024, 1], P('exp', 'ctx'), may hold values from 0 to 15; in each aligned block of 64 rows (0 to 63, 64 to 127, ..., all dimensions but the last counted through in order) at most 5 rows name the same one
- gate_weight: bfloat16 [16, 5120, 4096], P('exp', None, 'ctx'), may hold values from -0.078125 to 0.078125
- up_weight: bfloat16 [16, 5120, 4096], P('exp', None, 'ctx'), may hold values from -0.078125 to 0.078125
- down_weight: bfloat16 [16, 4096, 5120], P('exp', 'ctx'), may hold values from -0.375 to 0.375
Outputs:
- layer_out: bfloat16 [16, 1024, 5120], P('exp', 'ctx')
The draws below stay inside these ranges and needn't reach their ends.
Inputs may be any that keep to these rules, and one draw needn't show every extreme that they name: `expert_ids`: among the 64 positions p = c * 64 .. c * 64 + 63 of one sequence, for any c, no expert is named more than 5 times.
All inputs are finite; a program needn't handle non-finite values.
Results may differ from the reference program's by a relative error of at most 0.017.
Values may be sent and summed in bfloat16 or wider, within the bound.
No kernel may reach another device: no remote copies, remote signals or barrier semaphores. Data moves between devices by JAX's collectives and lax.ppermute only.
A program may use at most 128 MiB of HBM per device.

```python
import math
import jax
import jax.numpy as jnp
import numpy as np
from jax import lax

D = 5120
QUERY_HEADS = 20
KEY_VALUE_HEADS = 4
HEAD_SIZE = 128
FF = 4096
TOK_DEV = 64
DOCS = 4
EXPERTS = 16
SEQUENCE_COUNT = 16
SEQUENCE_LENGTH = 1024
QW = 2560
KW = 512
CAP = 5
N_CTX = 16


def draw_queries(key, part):
    sampled_values = jax.random.truncated_normal(jax.random.fold_in(key, 1), -4.5, 4.5, (SEQUENCE_COUNT, SEQUENCE_LENGTH, QUERY_HEADS * HEAD_SIZE), jnp.float32)
    return sampled_values.astype(jnp.bfloat16)


def draw_keys(key, part):
    sampled_values = jax.random.truncated_normal(jax.random.fold_in(key, 2), -4.5, 4.5, (SEQUENCE_COUNT, SEQUENCE_LENGTH, KEY_VALUE_HEADS * HEAD_SIZE), jnp.float32)
    return sampled_values.astype(jnp.bfloat16)


def level_of(own_key, shape, cuts, smallest, top_value):
    factor_of, own = 1.0, jax.random.fold_in(own_key, 6)
    for axis_at, blocks in cuts:
        steps = jnp.exp(jax.random.uniform(jax.random.fold_in(own, axis_at), (blocks,), jnp.float32, smallest / len(cuts), top_value / len(cuts)))
        factor_of = factor_of * jnp.repeat(steps, shape[axis_at] // blocks).reshape([-1 if axis == axis_at else 1 for axis in range(len(shape))])
    return factor_of


def profile(number_of, total, most, lean):
    portions = [(1 << 20) // math.isqrt(standing ** lean) + 1 for standing in range(2, number_of + 1)]
    surplus, given = total - most - (number_of - 1), [1] * (number_of - 1)
    while surplus > 0:
        free = [i for i in range(number_of - 1) if given[i] < most]
        mass, budget = sum([portions[i] for i in free]), surplus
        for i in free:
            extra = min(most - given[i], max(1, budget * portions[i] // mass), surplus)
            given[i] = given[i] + extra
            surplus = surplus - extra
    return np.array([most] + given)


def uneven_parts(own_key, amount, total, bound, lean):
    if amount == 2:
        one = jax.random.randint(own_key, (), max(1, total - bound), min(bound, total - 1) + 1)
        return jnp.stack([one, total - one])
    sizes = jnp.asarray(profile(amount, total, bound, lean), jnp.int32)
    couples = (amount - 1) // 2
    donor, receiver = sizes[1:1 + 2 * couples:2], sizes[2:2 + 2 * couples:2]
    room = jnp.minimum(donor - 1, bound - receiver)
    passed = jax.random.randint(jax.random.fold_in(own_key, 1), (couples,), 0, 1 << 20) % (room + 1)
    sizes = sizes.at[1:1 + 2 * couples:2].set(donor - passed).at[2:2 + 2 * couples:2].set(receiver + passed)
    return sizes[jax.random.permutation(jax.random.fold_in(own_key, 2), amount)]


def shared_out(stream_key, own, number, rows, count, top, limit, skew):
    ranking = jax.random.permutation(stream_key, count)
    heavy_load, common = portions_of(count, rows * top, limit, skew, True), portions_of(count, rows * top, limit, skew, False)
    places = jnp.arange(count)

    def named(sizes, rotation):
        used = int((sizes > 0).sum())
        fixed = max(1, used // 4)
        moved = fixed + (places - fixed + rotation * (used - fixed)) % max(1, count - fixed)
        return jnp.zeros((count,), jnp.int32).at[ranking[jnp.where(places < fixed, places, moved)]].set(jnp.asarray(sizes, jnp.int32))

    sizes = jnp.where(number % 4 == 0, named(heavy_load, number // 4), named(common, number - number // 4 - 1))
    mixed = jax.random.permutation(jax.random.fold_in(own, 3), count)
    source_of, sink = mixed[0:count // 2 * 2:2], mixed[1:count // 2 * 2:2]
    margin = jnp.minimum(sizes[source_of] - 1, limit - sizes[sink]) // 2
    margin = jnp.where((source_of == ranking[0]) | (sink == ranking[0]) | (sizes[sink] == 0), 0, jnp.maximum(margin, 0))
    moved = jax.random.randint(jax.random.fold_in(own, 4), (count // 2,), 0, 1 << 20) % (margin + 1)
    sizes = sizes.at[source_of].add(-moved).at[sink].add(moved)
    labels = jnp.searchsorted(jnp.cumsum(sizes), jnp.arange(rows * top), side="right").astype(jnp.int32)
    listing = labels.reshape(top, rows).T
    listing = listing[jax.random.permutation(jax.random.fold_in(own, 1), rows)]
    rotation = jax.random.randint(jax.random.fold_in(own, 2), (rows, 1), 0, top)
    return jnp.take_along_axis(listing, (jnp.arange(top)[None, :] + rotation) % top, axis=1)


def portions_of(amount, total, limit, lean, full):
    weights = [(1 << 20) // math.isqrt(standing ** lean) + 1 for standing in range(1, amount + 1)]
    largest = limit if full else min(limit, max(-(-total // amount), total * weights[0] // sum(weights)))
    least = 1 if total - largest >= amount - 1 else 0
    counts, spare = [largest] + [least] * (amount - 1), total - largest - least * (amount - 1)
    while spare > 0:
        free = [i for i in range(1, amount) if counts[i] < largest] or [i for i in range(1, amount) if counts[i] < limit]
        pool, left = sum([weights[i] for i in free]), spare
        for i in free:
            more = min(limit - counts[i], max(1, left * weights[i] // pool), spare)
            counts[i] = counts[i] + more
            spare = spare - more
    return np.array(counts)


def centred(key, dims, deviation, bound, shards=(), kind=jnp.bfloat16):
    level = level_of(key, dims, shards, -0.22, 0.18) if shards else 1.0
    result = jax.random.normal(key, dims, jnp.float32) * deviation * level
    return jnp.minimum(jnp.maximum(result, -bound), bound).astype(kind)


def setup_inputs(seed: int = 0) -> dict:
    key_list = jax.random.split(jax.random.key(seed), 13)
    queries = draw_queries(jax.random.fold_in(key_list[12], 71), 0)
    keys = draw_keys(jax.random.fold_in(key_list[12], 71), 0)
    values = centred(key_list[2], (SEQUENCE_COUNT, SEQUENCE_LENGTH, KW), 1.0, 6.0, ((0, 16), (1, 16)))
    doc_lengths = jax.vmap(lambda own: uneven_parts(own, DOCS, SEQUENCE_LENGTH, SEQUENCE_LENGTH // 2, 2))(jax.random.split(key_list[3], SEQUENCE_COUNT)).reshape((SEQUENCE_COUNT, DOCS)).astype(jnp.int32)
    resid = centred(key_list[4], (SEQUENCE_COUNT, SEQUENCE_LENGTH, D), 1.0, 6.0, ((0, 16), (1, 16)))
    out_weight = centred(key_list[5], (QW, D), (QW // 64) ** -0.5, 1.0, ((0, 256),))
    norm_gain = jnp.clip(1.0 + 0.18 * jax.random.normal(key_list[6], (D,), jnp.float32), 0.099609375, 1.8984375).astype(jnp.bfloat16)
    router_weight = centred(key_list[7], (D, EXPERTS), D ** -0.5, 0.078125)
    expert_ids_keys = jax.random.split(jax.random.fold_in(key_list[8], 1), SEQUENCE_COUNT * SEQUENCE_LENGTH // TOK_DEV)
    expert_ids_turns = jax.random.permutation(jax.random.fold_in(key_list[8], 3), SEQUENCE_COUNT * SEQUENCE_LENGTH // TOK_DEV)
    expert_ids = jax.vmap(lambda own, number: shared_out(jax.random.fold_in(key_list[8], 2), own, number, TOK_DEV, EXPERTS, 1, CAP, 2))(expert_ids_keys, expert_ids_turns).reshape((SEQUENCE_COUNT, SEQUENCE_LENGTH, 1))
    gate_weight = centred(key_list[9], (EXPERTS, D, FF), D ** -0.5, 0.078125, ((0, 16), (2, 16)))
    up_weight = centred(key_list[10], (EXPERTS, D, FF), D ** -0.5, 0.078125, ((0, 16), (2, 16)))
    down_weight = centred(key_list[11], (EXPERTS, FF, D), (FF // 16) ** -0.5, 0.375, ((0, 16), (1, 16)))
    return dict(queries=queries, keys=keys, values=values, doc_lengths=doc_lengths, resid=resid, out_weight=out_weight, norm_gain=norm_gain, router_weight=router_weight, expert_ids=expert_ids, gate_weight=gate_weight, up_weight=up_weight, down_weight=down_weight)


def doc_number(positions, lengths):
    bounds = jnp.cumsum(lengths).astype(jnp.int32)
    return lax.optimization_barrier(jnp.sum((positions[:, None] >= bounds[None, :]).astype(jnp.int32), axis=1)).astype(jnp.int32)

def attend_sequence(inputs):
    rows_of_query, rows_of_key, rows_of_value, lengths = inputs
    head_groups = QUERY_HEADS // KEY_VALUE_HEADS
    positions = jnp.arange(SEQUENCE_LENGTH, dtype=jnp.int32)
    documents = doc_number(positions, lengths)
    heads_of_query = rows_of_query.astype(jnp.float32).reshape(SEQUENCE_LENGTH, KEY_VALUE_HEADS, head_groups, HEAD_SIZE)
    heads_of_key = rows_of_key.astype(jnp.float32).reshape(SEQUENCE_LENGTH, KEY_VALUE_HEADS, HEAD_SIZE)
    heads_of_value = rows_of_value.astype(jnp.float32).reshape(SEQUENCE_LENGTH, KEY_VALUE_HEADS, HEAD_SIZE)
    scores = jnp.einsum('tkgd,nkd->kgtn', heads_of_query, heads_of_key) * (1.0 / jnp.sqrt(jnp.float32(HEAD_SIZE)))
    visible = (positions[None, :] <= positions[:, None]) & (documents[None, :] == documents[:, None])
    masked = jnp.where(visible, scores, -1e+30)
    top = lax.optimization_barrier(jnp.max(masked, axis=-1))
    weights = jnp.where(visible, jnp.exp(masked - top[..., None]), 0.0)
    total = lax.optimization_barrier(jnp.sum(weights, axis=-1))
    rounded = weights.astype(jnp.bfloat16).astype(jnp.float32)
    summed = jnp.einsum('kgtn,nkd->kgtd', rounded, heads_of_value)
    attended = summed / total[..., None]
    return attended.transpose(2, 0, 1, 3).reshape(SEQUENCE_LENGTH, QUERY_HEADS * HEAD_SIZE).astype(jnp.bfloat16)

def run_expert(inputs):
    gate_block, up_block, down_block, rows = inputs
    gate = jnp.dot(rows, gate_block, preferred_element_type=jnp.float32)
    up = jnp.dot(rows, up_block, preferred_element_type=jnp.float32)
    inner = (jax.nn.silu(gate) * up).astype(jnp.bfloat16)
    group_width = FF // N_CTX
    total = jnp.zeros((rows.shape[0], D), jnp.float32)
    for group in range(N_CTX):
        part = jnp.dot(inner[:, group * group_width:(group + 1) * group_width], down_block[group * group_width:(group + 1) * group_width], preferred_element_type=jnp.float32).astype(jnp.bfloat16)
        part = lax.optimization_barrier(part)
        total = total + part.astype(jnp.float32)
    return total.astype(jnp.bfloat16)

def reference(queries, keys, values, doc_lengths, resid, out_weight, norm_gain, router_weight, expert_ids, gate_weight, up_weight, down_weight):
    attended = lax.map(attend_sequence, (queries, keys, values, doc_lengths))
    flat = attended.reshape(SEQUENCE_COUNT * SEQUENCE_LENGTH, QUERY_HEADS * HEAD_SIZE)
    attn_proj = jnp.dot(flat, out_weight, preferred_element_type=jnp.float32).astype(jnp.bfloat16)
    hidden_state = resid.reshape(SEQUENCE_COUNT * SEQUENCE_LENGTH, D).astype(jnp.float32) + attn_proj.astype(jnp.float32)
    mean_square = lax.optimization_barrier(jnp.mean(hidden_state * hidden_state, axis=-1, keepdims=True))
    normed = hidden_state * lax.rsqrt(mean_square + 1e-05) * norm_gain.astype(jnp.float32)
    normed_b = normed.astype(jnp.bfloat16)
    logits = jnp.dot(normed_b, router_weight, preferred_element_type=jnp.float32)
    chosen = expert_ids.reshape(SEQUENCE_COUNT * SEQUENCE_LENGTH).astype(jnp.int32)
    picked = chosen[:, None] == jnp.arange(EXPERTS, dtype=jnp.int32)[None, :]
    score = jax.nn.sigmoid(lax.optimization_barrier(jnp.sum(jnp.where(picked, logits, 0.0), axis=-1)))
    routed = (normed * score[:, None]).astype(jnp.bfloat16)
    blocks = chosen.reshape(SEQUENCE_COUNT, N_CTX, TOK_DEV)
    onehot = (blocks[..., None] == jnp.arange(EXPERTS, dtype=jnp.int32)).astype(jnp.int32)
    earlier = (jnp.cumsum(onehot, axis=2) - onehot).astype(jnp.int32)
    slot_rank = lax.optimization_barrier(jnp.sum(earlier * onehot, axis=-1)).astype(jnp.int32)
    seq_index = jnp.arange(SEQUENCE_COUNT, dtype=jnp.int32)[:, None, None]
    ctx_index = jnp.arange(N_CTX, dtype=jnp.int32)[None, :, None]
    buffers = jnp.zeros((EXPERTS, SEQUENCE_COUNT, N_CTX, CAP, D), jnp.bfloat16)
    buffers = buffers.at[blocks, seq_index, ctx_index, slot_rank].set(routed.reshape(SEQUENCE_COUNT, N_CTX, TOK_DEV, D))
    results = lax.map(run_expert, (gate_weight, up_weight, down_weight, buffers.reshape(EXPERTS, SEQUENCE_COUNT * N_CTX * CAP, D)))
    results = results.reshape(EXPERTS, SEQUENCE_COUNT, N_CTX, CAP, D)
    expert_out = results[blocks, seq_index, ctx_index, slot_rank]
    layer_out = hidden_state + expert_out.reshape(SEQUENCE_COUNT * SEQUENCE_LENGTH, D).astype(jnp.float32)
    return layer_out.astype(jnp.bfloat16).reshape(SEQUENCE_COUNT, SEQUENCE_LENGTH, D)
```

```python
import math

import jax
import jax.numpy as jnp
from jax import lax
from jax.sharding import Mesh
from jax.sharding import PartitionSpec as P

HEAD_SIZE = 128
CTX = ("x", "zh", "core")
EXP = ("zl", "y")


def doc_number(positions, bounds):
    return jnp.sum((positions[:, None] >= bounds[None, :]).astype(jnp.int32), axis=1)


def _pp(v, axis, n, shift):
    return lax.ppermute(v, axis, [(i, (i + shift) % n) for i in range(n)])


def rel_index():
    x = lax.axis_index("x")
    zh = lax.axis_index("zh")
    c = lax.axis_index("core")
    dx = jnp.array([0, 0, -1, -1, 1, 1, -2, -2], jnp.int32)
    other_z = jnp.array([0, 1, 0, 1, 0, 1, 0, 1], jnp.int32)
    xs = (x + dx) % 4
    zs = (zh + other_z) % 2
    col = xs * 4 + zs * 2
    return jnp.concatenate([col + c, col + (1 - c)])


def ag_rel(b):
    zo = _pp(b, "zh", 2, 1)
    l1 = _pp(b, "x", 4, 1)
    r1 = _pp(b, "x", 4, -1)
    l1o = _pp(zo, "x", 4, 1)
    r1o = _pp(zo, "x", 4, -1)
    l2 = _pp(l1, "x", 4, 1)
    r2o = _pp(r1o, "x", 4, -1)
    first = jnp.concatenate([b, zo, l1, l1o, r1, r1o], 0)
    last = jnp.concatenate([l2, r2o], 0)
    return jnp.concatenate([first, last, _pp(first, "core", 2, 1), _pp(last, "core", 2, 1)], 0)


def rs_rel(p):
    r = p.shape[0] // 16
    got = _pp(p[8 * r:], "core", 2, 1).astype(jnp.float32)
    s = p[: 8 * r].astype(jnp.float32) + got
    blk = [s[i * r:(i + 1) * r] for i in range(8)]
    a = _pp(blk[6].astype(jnp.bfloat16), "x", 4, -1)
    b = _pp(blk[7].astype(jnp.bfloat16), "x", 4, 1)
    s2 = blk[2] + a.astype(jnp.float32)
    s5 = blk[5] + b.astype(jnp.float32)
    to_left = jnp.concatenate([s2, blk[3]], 0).astype(jnp.bfloat16)
    to_right = jnp.concatenate([blk[4], s5], 0).astype(jnp.bfloat16)
    from_right = _pp(to_left, "x", 4, -1).astype(jnp.float32)
    from_left = _pp(to_right, "x", 4, 1).astype(jnp.float32)
    t = jnp.concatenate([blk[0], blk[1]], 0) + from_right + from_left
    z = _pp(t[r:].astype(jnp.bfloat16), "zh", 2, 1).astype(jnp.float32)
    return t[:r] + z


def local(
    queries,
    keys,
    values,
    doc_lengths,
    resid,
    out_weight,
    norm_gain,
    router_weight,
    expert_ids,
    gate_weight,
    up_weight,
    down_weight,
):
    tok_rows = queries.shape[1]
    width = resid.shape[2]
    n_ctx = 16
    n_exp = 16
    my_ctx = lax.axis_index("x") * 4 + lax.axis_index("zh") * 2 + lax.axis_index("core")
    positions = my_ctx * tok_rows + jnp.arange(tok_rows, dtype=jnp.int32)
    bounds = jnp.cumsum(doc_lengths[0])
    query_doc = doc_number(positions, bounds)
    kv_heads = keys.shape[2] // HEAD_SIZE
    kw = keys.shape[2]
    head_groups = queries.shape[2] // keys.shape[2]
    heads_of_query = queries[0].reshape(tok_rows, kv_heads, head_groups, HEAD_SIZE)
    scale = 1.0 / math.sqrt(HEAD_SIZE)
    order = rel_index()
    kv_piece = ag_rel(jnp.concatenate([keys[0], values[0]], axis=1))
    key_piece = kv_piece[:, :kw]
    value_piece = kv_piece[:, kw:]
    count = key_piece.shape[0]
    heads_of_key = key_piece.reshape(count, kv_heads, HEAD_SIZE)
    heads_of_value = value_piece.reshape(count, kv_heads, HEAD_SIZE)
    scores = (
        jnp.einsum(
            "tkgd,nkd->kgtn", heads_of_query, heads_of_key, preferred_element_type=jnp.float32
        )
        * scale
    )
    key_pos = (order[:, None] * tok_rows + jnp.arange(tok_rows, dtype=jnp.int32)[None, :]).reshape(-1)
    visible = (key_pos[None, :] <= positions[:, None]) & (
        doc_number(key_pos, bounds)[None, :] == query_doc[:, None]
    )
    masked = jnp.where(visible, scores, -1e30)
    best = jnp.max(masked, axis=-1)
    weights = jnp.where(visible, jnp.exp(masked - best[..., None]), 0.0)
    total = jnp.sum(weights, axis=-1)
    accum = jnp.einsum(
        "kgtn,nkd->kgtd",
        weights.astype(jnp.bfloat16),
        heads_of_value,
        preferred_element_type=jnp.float32,
    )
    attended = (
        (accum / total[..., None]).transpose(2, 0, 1, 3).reshape(tok_rows, -1).astype(jnp.bfloat16)
    )
    qwidth = attended.shape[1]
    proj_rows = lax.all_gather(out_weight, EXP, axis=0, tiled=True)
    feature_block = lax.all_to_all(
        attended.reshape(tok_rows, n_ctx, qwidth // n_ctx),
        CTX,
        split_axis=1,
        concat_axis=0,
        tiled=True,
    )
    feature_rows = jnp.take(
        feature_block.reshape(n_ctx, tok_rows, -1), order, axis=0
    ).reshape(n_ctx * tok_rows, -1)
    attn_sum = rs_rel(
        jnp.dot(feature_rows, proj_rows, preferred_element_type=jnp.float32).astype(jnp.bfloat16)
    )
    hidden_state = resid[0].astype(jnp.float32) + attn_sum.astype(jnp.bfloat16).astype(jnp.float32)
    mean_square = jnp.mean(hidden_state * hidden_state, axis=-1, keepdims=True)
    normed = hidden_state * lax.rsqrt(mean_square + 1e-05) * norm_gain.astype(jnp.float32)
    normed_b = normed.astype(jnp.bfloat16)
    logits = jnp.dot(normed_b, router_weight, preferred_element_type=jnp.float32)
    n_experts = router_weight.shape[1]
    chosen = expert_ids[0, :, 0]
    picked = chosen[:, None] == jnp.arange(n_experts, dtype=jnp.int32)[None, :]
    score = jax.nn.sigmoid(jnp.sum(jnp.where(picked, logits, 0.0), axis=-1))
    routed = (normed * score[:, None]).astype(jnp.bfloat16)
    capacity = max(2, tok_rows // n_experts + tok_rows // (4 * n_experts))
    lower = jnp.tril(jnp.ones((tok_rows, tok_rows), jnp.float32), -1)
    earlier = jnp.dot(lower, picked.astype(jnp.float32), preferred_element_type=jnp.float32)
    slot_rank = jnp.sum(jnp.where(picked, earlier, 0.0), axis=-1).astype(jnp.int32)
    selector = picked[:, :, None] & (
        slot_rank[:, None, None] == jnp.arange(capacity, dtype=jnp.int32)[None, None, :]
    )
    selector_b = selector.astype(jnp.bfloat16)
    outgoing = jnp.einsum(
        "tes,td->esd", selector_b, routed, preferred_element_type=jnp.float32
    ).astype(jnp.bfloat16)
    arrived = lax.all_to_all(outgoing, EXP, split_axis=0, concat_axis=0, tiled=True)
    arrived_rows = arrived.reshape(-1, width)
    gate_local = gate_weight[0]
    up_local = up_weight[0]
    down_local = down_weight[0]
    piece = ag_rel(arrived_rows)
    gate = jnp.dot(piece, gate_local, preferred_element_type=jnp.float32)
    up = jnp.dot(piece, up_local, preferred_element_type=jnp.float32)
    inner = (jax.nn.silu(gate) * up).astype(jnp.bfloat16)
    summed = rs_rel(
        jnp.dot(inner, down_local, preferred_element_type=jnp.float32).astype(jnp.bfloat16)
    ).astype(jnp.bfloat16)
    expert_out = summed.reshape(n_exp, capacity, width)
    returned = lax.all_to_all(expert_out, EXP, split_axis=0, concat_axis=0, tiled=True)
    combined = jnp.einsum("tes,esd->td", selector_b, returned, preferred_element_type=jnp.float32)
    layer_out = (hidden_state + combined).astype(jnp.bfloat16)
    return layer_out[None]


def solution(mesh):
    fine = Mesh(mesh.devices.reshape(4, 2, 2, 4, 4), CTX + EXP)
    in_specs = (
        P(EXP, CTX, None),
        P(EXP, CTX, None),
        P(EXP, CTX, None),
        P(EXP, None),
        P(EXP, CTX, None),
        P(CTX + EXP, None),
        P(),
        P(),
        P(EXP, CTX, None),
        P(EXP, None, CTX),
        P(EXP, None, CTX),
        P(EXP, CTX, None),
    )
    out_specs = P(EXP, CTX, None)
    return jax.shard_map(local, mesh=fine, in_specs=in_specs, out_specs=out_specs, check_vma=False)
```

```python
import math

import jax
import jax.numpy as jnp
from jax import lax
from jax.sharding import Mesh
from jax.sharding import PartitionSpec as P

HEAD_SIZE = 128
CTX = ("x", "zh", "core")
EXP = ("zl", "y")


def doc_number(positions, bounds):
    return jnp.sum((positions[:, None] >= bounds[None, :]).astype(jnp.int32), axis=1)


def _pp(v, axis, n, shift):
    return lax.ppermute(v, axis, [(i, (i + shift) % n) for i in range(n)])


def rel_index():
    x = lax.axis_index("x")
    zh = lax.axis_index("zh")
    c = lax.axis_index("core")
    dx = jnp.array([0, 0, -1, -1, 1, 1, -2, -2], jnp.int32)
    other_z = jnp.array([0, 1, 0, 1, 0, 1, 0, 1], jnp.int32)
    xs = (x + dx) % 4
    zs = (zh + other_z) % 2
    col = xs * 4 + zs * 2
    return jnp.concatenate([col + c, col + (1 - c)])


def ag_rel(b):
    zo = _pp(b, "zh", 2, 1)
    l1 = _pp(b, "x", 4, 1)
    r1 = _pp(b, "x", 4, -1)
    l1o = _pp(zo, "x", 4, 1)
    r1o = _pp(zo, "x", 4, -1)
    l2 = _pp(l1, "x", 4, 1)
    r2o = _pp(r1o, "x", 4, -1)
    first = jnp.concatenate([b, zo, l1, l1o, r1, r1o], 0)
    last = jnp.concatenate([l2, r2o], 0)
    return jnp.concatenate([first, last, _pp(first, "core", 2, 1), _pp(last, "core", 2, 1)], 0)


def rs_rel(p):
    r = p.shape[0] // 16
    got = _pp(p[8 * r:], "core", 2, 1).astype(jnp.float32)
    s = p[: 8 * r].astype(jnp.float32) + got
    blk = [s[i * r:(i + 1) * r] for i in range(8)]
    a = _pp(blk[6].astype(jnp.bfloat16), "x", 4, -1)
    b = _pp(blk[7].astype(jnp.bfloat16), "x", 4, 1)
    s2 = blk[2] + a.astype(jnp.float32)
    s5 = blk[5] + b.astype(jnp.float32)
    to_left = jnp.concatenate([s2, blk[3]], 0).astype(jnp.bfloat16)
    to_right = jnp.concatenate([blk[4], s5], 0).astype(jnp.bfloat16)
    from_right = _pp(to_left, "x", 4, -1).astype(jnp.float32)
    from_left = _pp(to_right, "x", 4, 1).astype(jnp.float32)
    t = jnp.concatenate([blk[0], blk[1]], 0) + from_right + from_left
    z = _pp(t[r:].astype(jnp.bfloat16), "zh", 2, 1).astype(jnp.float32)
    return t[:r] + z


def a2a_send(out_rel):
    g = out_rel.reshape(4, 4, *out_rel.shape[1:])
    cols = [g[:, 0]] + [_pp(g[:, dy], "y", 4, dy) for dy in range(1, 4)]
    m = jnp.stack(cols, 1)
    rows = [m[0]] + [_pp(m[dz], "zl", 4, dz) for dz in range(1, 4)]
    return jnp.stack(rows, 0).reshape(out_rel.shape)


def a2a_back(res_rel):
    g = res_rel.reshape(4, 4, *res_rel.shape[1:])
    rows = [g[0]] + [_pp(g[dz], "zl", 4, -dz) for dz in range(1, 4)]
    n = jnp.stack(rows, 0)
    cols = [n[:, 0]] + [_pp(n[:, dy], "y", 4, -dy) for dy in range(1, 4)]
    return jnp.stack(cols, 1).reshape(res_rel.shape)


def local(
    queries,
    keys,
    values,
    doc_lengths,
    resid,
    out_weight,
    norm_gain,
    router_weight,
    expert_ids,
    gate_weight,
    up_weight,
    down_weight,
):
    tok_rows = queries.shape[1]
    width = resid.shape[2]
    n_ctx = 16
    n_exp = 16
    my_ctx = lax.axis_index("x") * 4 + lax.axis_index("zh") * 2 + lax.axis_index("core")
    positions = my_ctx * tok_rows + jnp.arange(tok_rows, dtype=jnp.int32)
    bounds = jnp.cumsum(doc_lengths[0])
    query_doc = doc_number(positions, bounds)
    kv_heads = keys.shape[2] // HEAD_SIZE
    kw = keys.shape[2]
    head_groups = queries.shape[2] // keys.shape[2]
    heads_of_query = queries[0].reshape(tok_rows, kv_heads, head_groups, HEAD_SIZE)
    scale = 1.0 / math.sqrt(HEAD_SIZE)
    order = rel_index()
    kv_piece = ag_rel(jnp.concatenate([keys[0], values[0]], axis=1))
    key_piece = kv_piece[:, :kw]
    value_piece = kv_piece[:, kw:]
    count = key_piece.shape[0]
    heads_of_key = key_piece.reshape(count, kv_heads, HEAD_SIZE)
    heads_of_value = value_piece.reshape(count, kv_heads, HEAD_SIZE)
    scores = (
        jnp.einsum(
            "tkgd,nkd->kgtn", heads_of_query, heads_of_key, preferred_element_type=jnp.float32
        )
        * scale
    )
    key_pos = (order[:, None] * tok_rows + jnp.arange(tok_rows, dtype=jnp.int32)[None, :]).reshape(-1)
    visible = (key_pos[None, :] <= positions[:, None]) & (
        doc_number(key_pos, bounds)[None, :] == query_doc[:, None]
    )
    masked = jnp.where(visible, scores, -1e30)
    best = jnp.max(masked, axis=-1)
    weights = jnp.where(visible, jnp.exp(masked - best[..., None]), 0.0)
    total = jnp.sum(weights, axis=-1)
    accum = jnp.einsum(
        "kgtn,nkd->kgtd",
        weights.astype(jnp.bfloat16),
        heads_of_value,
        preferred_element_type=jnp.float32,
    )
    attended = (
        (accum / total[..., None]).transpose(2, 0, 1, 3).reshape(tok_rows, -1).astype(jnp.bfloat16)
    )
    qwidth = attended.shape[1]
    proj_rows = lax.all_gather(out_weight, EXP, axis=0, tiled=True)
    feature_block = lax.all_to_all(
        attended.reshape(tok_rows, n_ctx, qwidth // n_ctx),
        CTX,
        split_axis=1,
        concat_axis=0,
        tiled=True,
    )
    feature_rows = jnp.take(
        feature_block.reshape(n_ctx, tok_rows, -1), order, axis=0
    ).reshape(n_ctx * tok_rows, -1)
    attn_sum = rs_rel(
        jnp.dot(feature_rows, proj_rows, preferred_element_type=jnp.float32).astype(jnp.bfloat16)
    )
    hidden_state = resid[0].astype(jnp.float32) + attn_sum.astype(jnp.bfloat16).astype(jnp.float32)
    mean_square = jnp.mean(hidden_state * hidden_state, axis=-1, keepdims=True)
    normed = hidden_state * lax.rsqrt(mean_square + 1e-05) * norm_gain.astype(jnp.float32)
    normed_b = normed.astype(jnp.bfloat16)
    logits = jnp.dot(normed_b, router_weight, preferred_element_type=jnp.float32)
    n_experts = router_weight.shape[1]
    chosen = expert_ids[0, :, 0]
    shift = jnp.arange(n_experts, dtype=jnp.int32)
    expert_of_shift = ((lax.axis_index("zl") + shift // 4) % 4) * 4 + (lax.axis_index("y") + shift % 4) % 4
    picked = chosen[:, None] == expert_of_shift[None, :]
    score = jax.nn.sigmoid(jnp.sum(jnp.where(picked, logits[:, expert_of_shift], 0.0), axis=-1))
    routed = (normed * score[:, None]).astype(jnp.bfloat16)
    capacity = max(2, tok_rows // n_experts + tok_rows // (4 * n_experts))
    lower = jnp.tril(jnp.ones((tok_rows, tok_rows), jnp.float32), -1)
    earlier = jnp.dot(lower, picked.astype(jnp.float32), preferred_element_type=jnp.float32)
    slot_rank = jnp.sum(jnp.where(picked, earlier, 0.0), axis=-1).astype(jnp.int32)
    selector = picked[:, :, None] & (
        slot_rank[:, None, None] == jnp.arange(capacity, dtype=jnp.int32)[None, None, :]
    )
    selector_b = selector.astype(jnp.bfloat16)
    outgoing = jnp.einsum(
        "tes,td->esd", selector_b, routed, preferred_element_type=jnp.float32
    ).astype(jnp.bfloat16)
    arrived = a2a_send(outgoing)
    arrived_rows = arrived.reshape(-1, width)
    gate_local = gate_weight[0]
    up_local = up_weight[0]
    down_local = down_weight[0]
    piece = ag_rel(arrived_rows)
    gate = jnp.dot(piece, gate_local, preferred_element_type=jnp.float32)
    up = jnp.dot(piece, up_local, preferred_element_type=jnp.float32)
    inner = (jax.nn.silu(gate) * up).astype(jnp.bfloat16)
    summed = rs_rel(
        jnp.dot(inner, down_local, preferred_element_type=jnp.float32).astype(jnp.bfloat16)
    ).astype(jnp.bfloat16)
    expert_out = summed.reshape(n_exp, capacity, width)
    returned = a2a_back(expert_out)
    combined = jnp.einsum("tes,esd->td", selector_b, returned, preferred_element_type=jnp.float32)
    layer_out = (hidden_state + combined).astype(jnp.bfloat16)
    return layer_out[None]


def solution(mesh):
    fine = Mesh(mesh.devices.reshape(4, 2, 2, 4, 4), CTX + EXP)
    in_specs = (
        P(EXP, CTX, None),
        P(EXP, CTX, None),
        P(EXP, CTX, None),
        P(EXP, None),
        P(EXP, CTX, None),
        P(CTX + EXP, None),
        P(),
        P(),
        P(EXP, CTX, None),
        P(EXP, None, CTX),
        P(EXP, None, CTX),
        P(EXP, CTX, None),
    )
    out_specs = P(EXP, CTX, None)
    return jax.shard_map(local, mesh=fine, in_specs=in_specs, out_specs=out_specs, check_vma=False)
```

```python
import math

import jax
import jax.numpy as jnp
from jax import lax
from jax.sharding import Mesh
from jax.sharding import PartitionSpec as P

HEAD_SIZE = 128
CTX = ("x", "zh", "core")
EXP = ("zl", "y")


def doc_number(positions, bounds):
    return jnp.sum((positions[:, None] >= bounds[None, :]).astype(jnp.int32), axis=1)


def _pp(v, axis, n, shift):
    return lax.ppermute(v, axis, [(i, (i + shift) % n) for i in range(n)])


def rel_index():
    x = lax.axis_index("x")
    zh = lax.axis_index("zh")
    c = lax.axis_index("core")
    dx = jnp.array([0, 0, -1, -1, 1, 1, -2, -2], jnp.int32)
    other_z = jnp.array([0, 1, 0, 1, 0, 1, 0, 1], jnp.int32)
    xs = (x + dx) % 4
    zs = (zh + other_z) % 2
    col = xs * 4 + zs * 2
    return jnp.concatenate([col + c, col + (1 - c)])


def ag_rel(b):
    zo = _pp(b, "zh", 2, 1)
    l1 = _pp(b, "x", 4, 1)
    r1 = _pp(b, "x", 4, -1)
    l1o = _pp(zo, "x", 4, 1)
    r1o = _pp(zo, "x", 4, -1)
    l2 = _pp(l1, "x", 4, 1)
    r2o = _pp(r1o, "x", 4, -1)
    first = jnp.concatenate([b, zo, l1, l1o, r1, r1o], 0)
    last = jnp.concatenate([l2, r2o], 0)
    return jnp.concatenate([first, last, _pp(first, "core", 2, 1), _pp(last, "core", 2, 1)], 0)


def rs_rel(own, other):
    r = own.shape[0] // 8
    got = _pp(other, "core", 2, 1)
    blk = [own[i * r:(i + 1) * r].astype(jnp.float32) + got[i * r:(i + 1) * r].astype(jnp.float32) for i in range(8)]
    a = _pp(blk[6].astype(jnp.bfloat16), "x", 4, -1)
    b = _pp(blk[7].astype(jnp.bfloat16), "x", 4, 1)
    c = _pp(blk[3].astype(jnp.bfloat16), "x", 4, -1)
    d = _pp(blk[4].astype(jnp.bfloat16), "x", 4, 1)
    e = _pp((blk[5] + b.astype(jnp.float32)).astype(jnp.bfloat16), "x", 4, 1)
    f = _pp((blk[2] + a.astype(jnp.float32)).astype(jnp.bfloat16), "x", 4, -1)
    t1 = blk[1] + c.astype(jnp.float32) + e.astype(jnp.float32)
    z = _pp(t1.astype(jnp.bfloat16), "zh", 2, 1)
    t0 = blk[0] + f.astype(jnp.float32) + d.astype(jnp.float32)
    return t0 + z.astype(jnp.float32)


def local(
    queries,
    keys,
    values,
    doc_lengths,
    resid,
    out_weight,
    norm_gain,
    router_weight,
    expert_ids,
    gate_weight,
    up_weight,
    down_weight,
):
    tok_rows = queries.shape[1]
    width = resid.shape[2]
    n_ctx = 16
    n_exp = 16
    my_ctx = lax.axis_index("x") * 4 + lax.axis_index("zh") * 2 + lax.axis_index("core")
    positions = my_ctx * tok_rows + jnp.arange(tok_rows, dtype=jnp.int32)
    bounds = jnp.cumsum(doc_lengths[0])
    query_doc = doc_number(positions, bounds)
    kv_heads = keys.shape[2] // HEAD_SIZE
    kw = keys.shape[2]
    head_groups = queries.shape[2] // keys.shape[2]
    heads_of_query = queries[0].reshape(tok_rows, kv_heads, head_groups, HEAD_SIZE)
    scale = 1.0 / math.sqrt(HEAD_SIZE)
    order = rel_index()
    kv_piece = ag_rel(jnp.concatenate([keys[0], values[0]], axis=1))
    key_piece = kv_piece[:, :kw]
    value_piece = kv_piece[:, kw:]
    count = key_piece.shape[0]
    heads_of_key = key_piece.reshape(count, kv_heads, HEAD_SIZE)
    heads_of_value = value_piece.reshape(count, kv_heads, HEAD_SIZE)
    scores = (
        jnp.einsum(
            "tkgd,nkd->kgtn", heads_of_query, heads_of_key, preferred_element_type=jnp.float32
        )
        * scale
    )
    key_pos = (order[:, None] * tok_rows + jnp.arange(tok_rows, dtype=jnp.int32)[None, :]).reshape(-1)
    visible = (key_pos[None, :] <= positions[:, None]) & (
        doc_number(key_pos, bounds)[None, :] == query_doc[:, None]
    )
    masked = jnp.where(visible, scores, -1e30)
    best = jnp.max(masked, axis=-1)
    weights = jnp.where(visible, jnp.exp(masked - best[..., None]), 0.0)
    total = jnp.sum(weights, axis=-1)
    accum = jnp.einsum(
        "kgtn,nkd->kgtd",
        weights.astype(jnp.bfloat16),
        heads_of_value,
        preferred_element_type=jnp.float32,
    )
    attended = (
        (accum / total[..., None]).transpose(2, 0, 1, 3).reshape(tok_rows, -1).astype(jnp.bfloat16)
    )
    qwidth = attended.shape[1]
    proj_rows = lax.all_gather(out_weight, EXP, axis=0, tiled=True)
    feature_block = lax.all_to_all(
        attended.reshape(tok_rows, n_ctx, qwidth // n_ctx),
        CTX,
        split_axis=1,
        concat_axis=0,
        tiled=True,
    )
    feature_rows = jnp.take(
        feature_block.reshape(n_ctx, tok_rows, -1), order, axis=0
    ).reshape(n_ctx * tok_rows, -1)
    half = 8 * tok_rows
    attn_other = jnp.dot(feature_rows[half:], proj_rows, preferred_element_type=jnp.float32).astype(jnp.bfloat16)
    attn_own = jnp.dot(feature_rows[:half], proj_rows, preferred_element_type=jnp.float32).astype(jnp.bfloat16)
    attn_sum = rs_rel(attn_own, attn_other)
    hidden_state = resid[0].astype(jnp.float32) + attn_sum.astype(jnp.bfloat16).astype(jnp.float32)
    mean_square = jnp.mean(hidden_state * hidden_state, axis=-1, keepdims=True)
    normed = hidden_state * lax.rsqrt(mean_square + 1e-05) * norm_gain.astype(jnp.float32)
    normed_b = normed.astype(jnp.bfloat16)
    logits = jnp.dot(normed_b, router_weight, preferred_element_type=jnp.float32)
    n_experts = router_weight.shape[1]
    chosen = expert_ids[0, :, 0]
    picked = chosen[:, None] == jnp.arange(n_experts, dtype=jnp.int32)[None, :]
    score = jax.nn.sigmoid(jnp.sum(jnp.where(picked, logits, 0.0), axis=-1))
    routed = (normed * score[:, None]).astype(jnp.bfloat16)
    capacity = max(2, tok_rows // n_experts + tok_rows // (4 * n_experts))
    lower = jnp.tril(jnp.ones((tok_rows, tok_rows), jnp.float32), -1)
    earlier = jnp.dot(lower, picked.astype(jnp.float32), preferred_element_type=jnp.float32)
    slot_rank = jnp.sum(jnp.where(picked, earlier, 0.0), axis=-1).astype(jnp.int32)
    selector = picked[:, :, None] & (
        slot_rank[:, None, None] == jnp.arange(capacity, dtype=jnp.int32)[None, None, :]
    )
    selector_b = selector.astype(jnp.bfloat16)
    outgoing = jnp.einsum(
        "tes,td->esd", selector_b, routed, preferred_element_type=jnp.float32
    ).astype(jnp.bfloat16)
    arrived = lax.all_to_all(outgoing, EXP, split_axis=0, concat_axis=0, tiled=True)
    arrived_rows = arrived.reshape(-1, width)
    gate_local = gate_weight[0]
    up_local = up_weight[0]
    down_local = down_weight[0]
    piece = ag_rel(arrived_rows)
    rows_half = piece.shape[0] // 2

    def expert_rows(rows):
        gate = jnp.dot(rows, gate_local, preferred_element_type=jnp.float32)
        up = jnp.dot(rows, up_local, preferred_element_type=jnp.float32)
        inner = (jax.nn.silu(gate) * up).astype(jnp.bfloat16)
        return jnp.dot(inner, down_local, preferred_element_type=jnp.float32).astype(jnp.bfloat16)

    part_own = expert_rows(piece[:rows_half])
    part_other = expert_rows(piece[rows_half:])
    summed = rs_rel(part_own, part_other).astype(jnp.bfloat16)
    expert_out = summed.reshape(n_exp, capacity, width)
    returned = lax.all_to_all(expert_out, EXP, split_axis=0, concat_axis=0, tiled=True)
    combined = jnp.einsum("tes,esd->td", selector_b, returned, preferred_element_type=jnp.float32)
    layer_out = (hidden_state + combined).astype(jnp.bfloat16)
    return layer_out[None]


def solution(mesh):
    fine = Mesh(mesh.devices.reshape(4, 2, 2, 4, 4), CTX + EXP)
    in_specs = (
        P(EXP, CTX, None),
        P(EXP, CTX, None),
        P(EXP, CTX, None),
        P(EXP, None),
        P(EXP, CTX, None),
        P(CTX + EXP, None),
        P(),
        P(),
        P(EXP, CTX, None),
        P(EXP, None, CTX),
        P(EXP, None, CTX),
        P(EXP, CTX, None),
    )
    out_specs = P(EXP, CTX, None)
    return jax.shard_map(local, mesh=fine, in_specs=in_specs, out_specs=out_specs, check_vma=False)
```

```python
import math

import jax
import jax.numpy as jnp
from jax import lax
from jax.sharding import Mesh
from jax.sharding import PartitionSpec as P

HEAD_SIZE = 128
CTX = ("x", "zh", "core")
EXP = ("zl", "y")


def doc_number(positions, bounds):
    return jnp.sum((positions[:, None] >= bounds[None, :]).astype(jnp.int32), axis=1)


def _pp(v, axis, n, shift):
    return lax.ppermute(v, axis, [(i, (i + shift) % n) for i in range(n)])


def zswap(v):
    h = v.shape[0] // 2
    zz = ("zh", "zl")
    up = _pp(_pp(v[:h], zz, 8, 2), zz, 8, 2)
    down = _pp(_pp(v[h:], zz, 8, -2), zz, 8, -2)
    return jnp.concatenate([up, down], 0)


def rel_index():
    x = lax.axis_index("x")
    zh = lax.axis_index("zh")
    c = lax.axis_index("core")
    dx = jnp.array([0, 0, -1, -1, 1, 1, -2, -2], jnp.int32)
    other_z = jnp.array([0, 1, 0, 1, 0, 1, 0, 1], jnp.int32)
    xs = (x + dx) % 4
    zs = (zh + other_z) % 2
    col = xs * 4 + zs * 2
    return jnp.concatenate([col + c, col + (1 - c)])


def ag_rel(b):
    zo = zswap(b)
    l1 = _pp(b, "x", 4, 1)
    r1 = _pp(b, "x", 4, -1)
    l1o = _pp(zo, "x", 4, 1)
    r1o = _pp(zo, "x", 4, -1)
    l2 = _pp(l1, "x", 4, 1)
    r2o = _pp(r1o, "x", 4, -1)
    first = jnp.concatenate([b, zo, l1, l1o, r1, r1o], 0)
    last = jnp.concatenate([l2, r2o], 0)
    return jnp.concatenate([first, last, _pp(first, "core", 2, 1), _pp(last, "core", 2, 1)], 0)


def rs_rel(own, other):
    r = own.shape[0] // 8
    got = _pp(other, "core", 2, 1)
    blk = [own[i * r:(i + 1) * r].astype(jnp.float32) + got[i * r:(i + 1) * r].astype(jnp.float32) for i in range(8)]
    a = _pp(blk[6].astype(jnp.bfloat16), "x", 4, -1)
    b = _pp(blk[7].astype(jnp.bfloat16), "x", 4, 1)
    c = _pp(blk[3].astype(jnp.bfloat16), "x", 4, -1)
    d = _pp(blk[4].astype(jnp.bfloat16), "x", 4, 1)
    e = _pp((blk[5] + b.astype(jnp.float32)).astype(jnp.bfloat16), "x", 4, 1)
    f = _pp((blk[2] + a.astype(jnp.float32)).astype(jnp.bfloat16), "x", 4, -1)
    t1 = blk[1] + c.astype(jnp.float32) + e.astype(jnp.float32)
    z = zswap(t1.astype(jnp.bfloat16))
    t0 = blk[0] + f.astype(jnp.float32) + d.astype(jnp.float32)
    return t0 + z.astype(jnp.float32)


def local(
    queries,
    keys,
    values,
    doc_lengths,
    resid,
    out_weight,
    norm_gain,
    router_weight,
    expert_ids,
    gate_weight,
    up_weight,
    down_weight,
):
    tok_rows = queries.shape[1]
    width = resid.shape[2]
    n_ctx = 16
    n_exp = 16
    my_ctx = lax.axis_index("x") * 4 + lax.axis_index("zh") * 2 + lax.axis_index("core")
    positions = my_ctx * tok_rows + jnp.arange(tok_rows, dtype=jnp.int32)
    bounds = jnp.cumsum(doc_lengths[0])
    query_doc = doc_number(positions, bounds)
    kv_heads = keys.shape[2] // HEAD_SIZE
    kw = keys.shape[2]
    head_groups = queries.shape[2] // keys.shape[2]
    heads_of_query = queries[0].reshape(tok_rows, kv_heads, head_groups, HEAD_SIZE)
    scale = 1.0 / math.sqrt(HEAD_SIZE)
    order = rel_index()
    kv_piece = ag_rel(jnp.concatenate([keys[0], values[0]], axis=1))
    key_piece = kv_piece[:, :kw]
    value_piece = kv_piece[:, kw:]
    count = key_piece.shape[0]
    heads_of_key = key_piece.reshape(count, kv_heads, HEAD_SIZE)
    heads_of_value = value_piece.reshape(count, kv_heads, HEAD_SIZE)
    scores = (
        jnp.einsum(
            "tkgd,nkd->kgtn", heads_of_query, heads_of_key, preferred_element_type=jnp.float32
        )
        * scale
    )
    key_pos = (order[:, None] * tok_rows + jnp.arange(tok_rows, dtype=jnp.int32)[None, :]).reshape(-1)
    visible = (key_pos[None, :] <= positions[:, None]) & (
        doc_number(key_pos, bounds)[None, :] == query_doc[:, None]
    )
    masked = jnp.where(visible, scores, -1e30)
    best = jnp.max(masked, axis=-1)
    weights = jnp.where(visible, jnp.exp(masked - best[..., None]), 0.0)
    total = jnp.sum(weights, axis=-1)
    accum = jnp.einsum(
        "kgtn,nkd->kgtd",
        weights.astype(jnp.bfloat16),
        heads_of_value,
        preferred_element_type=jnp.float32,
    )
    attended = (
        (accum / total[..., None]).transpose(2, 0, 1, 3).reshape(tok_rows, -1).astype(jnp.bfloat16)
    )
    qwidth = attended.shape[1]
    proj_rows = lax.all_gather(out_weight, EXP, axis=0, tiled=True)
    feature_block = lax.all_to_all(
        attended.reshape(tok_rows, n_ctx, qwidth // n_ctx),
        CTX,
        split_axis=1,
        concat_axis=0,
        tiled=True,
    )
    feature_rows = jnp.take(
        feature_block.reshape(n_ctx, tok_rows, -1), order, axis=0
    ).reshape(n_ctx * tok_rows, -1)
    half = 8 * tok_rows
    attn_other = jnp.dot(feature_rows[half:], proj_rows, preferred_element_type=jnp.float32).astype(jnp.bfloat16)
    attn_own = jnp.dot(feature_rows[:half], proj_rows, preferred_element_type=jnp.float32).astype(jnp.bfloat16)
    attn_sum = rs_rel(attn_own, attn_other)
    hidden_state = resid[0].astype(jnp.float32) + attn_sum.astype(jnp.bfloat16).astype(jnp.float32)
    mean_square = jnp.mean(hidden_state * hidden_state, axis=-1, keepdims=True)
    normed = hidden_state * lax.rsqrt(mean_square + 1e-05) * norm_gain.astype(jnp.float32)
    normed_b = normed.astype(jnp.bfloat16)
    logits = jnp.dot(normed_b, router_weight, preferred_element_type=jnp.float32)
    n_experts = router_weight.shape[1]
    chosen = expert_ids[0, :, 0]
    picked = chosen[:, None] == jnp.arange(n_experts, dtype=jnp.int32)[None, :]
    score = jax.nn.sigmoid(jnp.sum(jnp.where(picked, logits, 0.0), axis=-1))
    routed = (normed * score[:, None]).astype(jnp.bfloat16)
    capacity = max(2, tok_rows // n_experts + tok_rows // (4 * n_experts))
    lower = jnp.tril(jnp.ones((tok_rows, tok_rows), jnp.float32), -1)
    earlier = jnp.dot(lower, picked.astype(jnp.float32), preferred_element_type=jnp.float32)
    slot_rank = jnp.sum(jnp.where(picked, earlier, 0.0), axis=-1).astype(jnp.int32)
    selector = picked[:, :, None] & (
        slot_rank[:, None, None] == jnp.arange(capacity, dtype=jnp.int32)[None, None, :]
    )
    selector_b = selector.astype(jnp.bfloat16)
    outgoing = jnp.einsum(
        "tes,td->esd", selector_b, routed, preferred_element_type=jnp.float32
    ).astype(jnp.bfloat16)
    arrived = lax.all_to_all(outgoing, EXP, split_axis=0, concat_axis=0, tiled=True)
    arrived_rows = arrived.reshape(-1, width)
    gate_local = gate_weight[0]
    up_local = up_weight[0]
    down_local = down_weight[0]
    piece = ag_rel(arrived_rows)
    rows_half = piece.shape[0] // 2

    def expert_rows(rows):
        gate = jnp.dot(rows, gate_local, preferred_element_type=jnp.float32)
        up = jnp.dot(rows, up_local, preferred_element_type=jnp.float32)
        inner = (jax.nn.silu(gate) * up).astype(jnp.bfloat16)
        return jnp.dot(inner, down_local, preferred_element_type=jnp.float32).astype(jnp.bfloat16)

    part_own = expert_rows(piece[:rows_half])
    part_other = expert_rows(piece[rows_half:])
    summed = rs_rel(part_own, part_other).astype(jnp.bfloat16)
    expert_out = summed.reshape(n_exp, capacity, width)
    returned = lax.all_to_all(expert_out, EXP, split_axis=0, concat_axis=0, tiled=True)
    combined = jnp.einsum("tes,esd->td", selector_b, returned, preferred_element_type=jnp.float32)
    layer_out = (hidden_state + combined).astype(jnp.bfloat16)
    return layer_out[None]


def solution(mesh):
    fine = Mesh(mesh.devices.reshape(4, 2, 2, 4, 4), CTX + EXP)
    in_specs = (
        P(EXP, CTX, None),
        P(EXP, CTX, None),
        P(EXP, CTX, None),
        P(EXP, None),
        P(EXP, CTX, None),
        P(CTX + EXP, None),
        P(),
        P(),
        P(EXP, CTX, None),
        P(EXP, None, CTX),
        P(EXP, None, CTX),
        P(EXP, CTX, None),
    )
    out_specs = P(EXP, CTX, None)
    return jax.shard_map(local, mesh=fine, in_specs=in_specs, out_specs=out_specs, check_vma=False)
```

```python
import math

import jax
import jax.numpy as jnp
from jax import lax
from jax.sharding import Mesh
from jax.sharding import PartitionSpec as P

HEAD_SIZE = 128
CTX = ("x", "zh", "core")
EXP = ("zl", "y")


def doc_number(positions, bounds):
    return jnp.sum((positions[:, None] >= bounds[None, :]).astype(jnp.int32), axis=1)


def _pp(v, axis, n, shift):
    return lax.ppermute(v, axis, [(i, (i + shift) % n) for i in range(n)])


def rel_index():
    x = lax.axis_index("x")
    zh = lax.axis_index("zh")
    c = lax.axis_index("core")
    dx = jnp.array([0, 0, -1, -1, 1, 1, -2, -2], jnp.int32)
    other_z = jnp.array([0, 1, 0, 1, 0, 1, 0, 1], jnp.int32)
    xs = (x + dx) % 4
    zs = (zh + other_z) % 2
    col = xs * 4 + zs * 2
    return jnp.concatenate([col + c, col + (1 - c)])


def ag_rel(b):
    zo = _pp(b, "zh", 2, 1)
    l1 = _pp(b, "x", 4, 1)
    r1 = _pp(b, "x", 4, -1)
    l1o = _pp(zo, "x", 4, 1)
    r1o = _pp(zo, "x", 4, -1)
    l2 = _pp(l1, "x", 4, 1)
    r2o = _pp(r1o, "x", 4, -1)
    first = jnp.concatenate([b, zo, l1, l1o, r1, r1o], 0)
    last = jnp.concatenate([l2, r2o], 0)
    return jnp.concatenate([first, last, _pp(first, "core", 2, 1), _pp(last, "core", 2, 1)], 0)


def rs_rel(own, other):
    r = own.shape[0] // 8
    got = _pp(other, "core", 2, 1)
    blk = [own[i * r:(i + 1) * r].astype(jnp.float32) + got[i * r:(i + 1) * r].astype(jnp.float32) for i in range(8)]
    ac = _pp(jnp.concatenate([blk[6], blk[3]], 0).astype(jnp.bfloat16), "x", 4, -1)
    bd = _pp(jnp.concatenate([blk[7], blk[4]], 0).astype(jnp.bfloat16), "x", 4, 1)
    a, c = ac[:r], ac[r:]
    b, d = bd[:r], bd[r:]
    e = _pp((blk[5] + b.astype(jnp.float32)).astype(jnp.bfloat16), "x", 4, 1)
    f = _pp((blk[2] + a.astype(jnp.float32)).astype(jnp.bfloat16), "x", 4, -1)
    t1 = blk[1] + c.astype(jnp.float32) + e.astype(jnp.float32)
    z = _pp(t1.astype(jnp.bfloat16), "zh", 2, 1)
    t0 = blk[0] + f.astype(jnp.float32) + d.astype(jnp.float32)
    return t0 + z.astype(jnp.float32)


def local(
    queries,
    keys,
    values,
    doc_lengths,
    resid,
    out_weight,
    norm_gain,
    router_weight,
    expert_ids,
    gate_weight,
    up_weight,
    down_weight,
):
    tok_rows = queries.shape[1]
    width = resid.shape[2]
    n_ctx = 16
    n_exp = 16
    my_ctx = lax.axis_index("x") * 4 + lax.axis_index("zh") * 2 + lax.axis_index("core")
    positions = my_ctx * tok_rows + jnp.arange(tok_rows, dtype=jnp.int32)
    bounds = jnp.cumsum(doc_lengths[0])
    query_doc = doc_number(positions, bounds)
    kv_heads = keys.shape[2] // HEAD_SIZE
    kw = keys.shape[2]
    head_groups = queries.shape[2] // keys.shape[2]
    heads_of_query = queries[0].reshape(tok_rows, kv_heads, head_groups, HEAD_SIZE)
    scale = 1.0 / math.sqrt(HEAD_SIZE)
    order = rel_index()
    kv_piece = ag_rel(jnp.concatenate([keys[0], values[0]], axis=1))
    key_piece = kv_piece[:, :kw]
    value_piece = kv_piece[:, kw:]
    count = key_piece.shape[0]
    heads_of_key = key_piece.reshape(count, kv_heads, HEAD_SIZE)
    heads_of_value = value_piece.reshape(count, kv_heads, HEAD_SIZE)
    scores = (
        jnp.einsum(
            "tkgd,nkd->kgtn", heads_of_query, heads_of_key, preferred_element_type=jnp.float32
        )
        * scale
    )
    key_pos = (order[:, None] * tok_rows + jnp.arange(tok_rows, dtype=jnp.int32)[None, :]).reshape(-1)
    visible = (key_pos[None, :] <= positions[:, None]) & (
        doc_number(key_pos, bounds)[None, :] == query_doc[:, None]
    )
    masked = jnp.where(visible, scores, -1e30)
    best = jnp.max(masked, axis=-1)
    weights = jnp.where(visible, jnp.exp(masked - best[..., None]), 0.0)
    total = jnp.sum(weights, axis=-1)
    accum = jnp.einsum(
        "kgtn,nkd->kgtd",
        weights.astype(jnp.bfloat16),
        heads_of_value,
        preferred_element_type=jnp.float32,
    )
    attended = (
        (accum / total[..., None]).transpose(2, 0, 1, 3).reshape(tok_rows, -1).astype(jnp.bfloat16)
    )
    qwidth = attended.shape[1]
    proj_rows = lax.all_gather(out_weight, EXP, axis=0, tiled=True)
    feature_block = lax.all_to_all(
        attended.reshape(tok_rows, n_ctx, qwidth // n_ctx),
        CTX,
        split_axis=1,
        concat_axis=0,
        tiled=True,
    )
    feature_rows = jnp.take(
        feature_block.reshape(n_ctx, tok_rows, -1), order, axis=0
    ).reshape(n_ctx * tok_rows, -1)
    half = 8 * tok_rows
    attn_other = jnp.dot(feature_rows[half:], proj_rows, preferred_element_type=jnp.float32).astype(jnp.bfloat16)
    attn_own = jnp.dot(feature_rows[:half], proj_rows, preferred_element_type=jnp.float32).astype(jnp.bfloat16)
    attn_sum = rs_rel(attn_own, attn_other)
    hidden_state = resid[0].astype(jnp.float32) + attn_sum.astype(jnp.bfloat16).astype(jnp.float32)
    mean_square = jnp.mean(hidden_state * hidden_state, axis=-1, keepdims=True)
    normed = hidden_state * lax.rsqrt(mean_square + 1e-05) * norm_gain.astype(jnp.float32)
    normed_b = normed.astype(jnp.bfloat16)
    logits = jnp.dot(normed_b, router_weight, preferred_element_type=jnp.float32)
    n_experts = router_weight.shape[1]
    chosen = expert_ids[0, :, 0]
    picked = chosen[:, None] == jnp.arange(n_experts, dtype=jnp.int32)[None, :]
    score = jax.nn.sigmoid(jnp.sum(jnp.where(picked, logits, 0.0), axis=-1))
    routed = (normed * score[:, None]).astype(jnp.bfloat16)
    capacity = max(2, tok_rows // n_experts + tok_rows // (4 * n_experts))
    lower = jnp.tril(jnp.ones((tok_rows, tok_rows), jnp.float32), -1)
    earlier = jnp.dot(lower, picked.astype(jnp.float32), preferred_element_type=jnp.float32)
    slot_rank = jnp.sum(jnp.where(picked, earlier, 0.0), axis=-1).astype(jnp.int32)
    selector = picked[:, :, None] & (
        slot_rank[:, None, None] == jnp.arange(capacity, dtype=jnp.int32)[None, None, :]
    )
    selector_b = selector.astype(jnp.bfloat16)
    outgoing = jnp.einsum(
        "tes,td->esd", selector_b, routed, preferred_element_type=jnp.float32
    ).astype(jnp.bfloat16)
    arrived = lax.all_to_all(outgoing, EXP, split_axis=0, concat_axis=0, tiled=True)
    arrived_rows = arrived.reshape(-1, width)
    gate_local = gate_weight[0]
    up_local = up_weight[0]
    down_local = down_weight[0]
    piece = ag_rel(arrived_rows)
    rows_half = piece.shape[0] // 2

    def expert_rows(rows):
        gate = jnp.dot(rows, gate_local, preferred_element_type=jnp.float32)
        up = jnp.dot(rows, up_local, preferred_element_type=jnp.float32)
        inner = (jax.nn.silu(gate) * up).astype(jnp.bfloat16)
        return jnp.dot(inner, down_local, preferred_element_type=jnp.float32).astype(jnp.bfloat16)

    part_own = expert_rows(piece[:rows_half])
    part_other = expert_rows(piece[rows_half:])
    summed = rs_rel(part_own, part_other).astype(jnp.bfloat16)
    expert_out = summed.reshape(n_exp, capacity, width)
    returned = lax.all_to_all(expert_out, EXP, split_axis=0, concat_axis=0, tiled=True)
    combined = jnp.einsum("tes,esd->td", selector_b, returned, preferred_element_type=jnp.float32)
    layer_out = (hidden_state + combined).astype(jnp.bfloat16)
    return layer_out[None]


def solution(mesh):
    fine = Mesh(mesh.devices.reshape(4, 2, 2, 4, 4), CTX + EXP)
    in_specs = (
        P(EXP, CTX, None),
        P(EXP, CTX, None),
        P(EXP, CTX, None),
        P(EXP, None),
        P(EXP, CTX, None),
        P(CTX + EXP, None),
        P(),
        P(),
        P(EXP, CTX, None),
        P(EXP, None, CTX),
        P(EXP, None, CTX),
        P(EXP, CTX, None),
    )
    out_specs = P(EXP, CTX, None)
    return jax.shard_map(local, mesh=fine, in_specs=in_specs, out_specs=out_specs, check_vma=False)
```

```python
import math

import jax
import jax.numpy as jnp
from jax import lax
from jax.sharding import Mesh
from jax.sharding import PartitionSpec as P

HEAD_SIZE = 128
CTX = ("x", "zh", "core")
EXP = ("zl", "y")


def doc_number(positions, bounds):
    return jnp.sum((positions[:, None] >= bounds[None, :]).astype(jnp.int32), axis=1)


def _pp(v, axis, n, shift):
    return lax.ppermute(v, axis, [(i, (i + shift) % n) for i in range(n)])


def rel_index():
    x = lax.axis_index("x")
    zh = lax.axis_index("zh")
    c = lax.axis_index("core")
    dx = jnp.array([0, 0, -1, -1, 1, 1, -2, -2], jnp.int32)
    other_z = jnp.array([0, 1, 0, 1, 0, 1, 0, 1], jnp.int32)
    xs = (x + dx) % 4
    zs = (zh + other_z) % 2
    col = xs * 4 + zs * 2
    return jnp.concatenate([col + c, col + (1 - c)])


def ag_rel(b):
    zo = _pp(b, "zh", 2, 1)
    l1 = _pp(b, "x", 4, 1)
    r1 = _pp(b, "x", 4, -1)
    l1o = _pp(zo, "x", 4, 1)
    r1o = _pp(zo, "x", 4, -1)
    l2 = _pp(l1, "x", 4, 1)
    r2o = _pp(r1o, "x", 4, -1)
    first = jnp.concatenate([b, zo, l1, l1o, r1, r1o], 0)
    last = jnp.concatenate([l2, r2o], 0)
    return jnp.concatenate([first, last, _pp(first, "core", 2, 1), _pp(last, "core", 2, 1)], 0)


def rs_rel(own, other):
    r = own.shape[0] // 8
    got = _pp(other, "core", 2, 1)
    blk = [own[i * r:(i + 1) * r].astype(jnp.float32) + got[i * r:(i + 1) * r].astype(jnp.float32) for i in range(8)]
    b = _pp(blk[7].astype(jnp.bfloat16), "x", 4, 1)
    c = _pp(blk[3].astype(jnp.bfloat16), "x", 4, -1)
    e = _pp((blk[5] + b.astype(jnp.float32)).astype(jnp.bfloat16), "x", 4, 1)
    a_src, _ = lax.optimization_barrier((blk[6].astype(jnp.bfloat16), c))
    a = _pp(a_src, "x", 4, -1)
    t1 = blk[1] + c.astype(jnp.float32) + e.astype(jnp.float32)
    z = _pp(t1.astype(jnp.bfloat16), "zh", 2, 1)
    d_src, _ = lax.optimization_barrier((blk[4].astype(jnp.bfloat16), e))
    d = _pp(d_src, "x", 4, 1)
    f = _pp((blk[2] + a.astype(jnp.float32)).astype(jnp.bfloat16), "x", 4, -1)
    t0 = blk[0] + f.astype(jnp.float32) + d.astype(jnp.float32)
    return t0 + z.astype(jnp.float32)


def local(
    queries,
    keys,
    values,
    doc_lengths,
    resid,
    out_weight,
    norm_gain,
    router_weight,
    expert_ids,
    gate_weight,
    up_weight,
    down_weight,
):
    tok_rows = queries.shape[1]
    width = resid.shape[2]
    n_ctx = 16
    n_exp = 16
    my_ctx = lax.axis_index("x") * 4 + lax.axis_index("zh") * 2 + lax.axis_index("core")
    positions = my_ctx * tok_rows + jnp.arange(tok_rows, dtype=jnp.int32)
    bounds = jnp.cumsum(doc_lengths[0])
    query_doc = doc_number(positions, bounds)
    kv_heads = keys.shape[2] // HEAD_SIZE
    kw = keys.shape[2]
    head_groups = queries.shape[2] // keys.shape[2]
    heads_of_query = queries[0].reshape(tok_rows, kv_heads, head_groups, HEAD_SIZE)
    scale = 1.0 / math.sqrt(HEAD_SIZE)
    order = rel_index()
    kv_piece = ag_rel(jnp.concatenate([keys[0], values[0]], axis=1))
    key_piece = kv_piece[:, :kw]
    value_piece = kv_piece[:, kw:]
    count = key_piece.shape[0]
    heads_of_key = key_piece.reshape(count, kv_heads, HEAD_SIZE)
    heads_of_value = value_piece.reshape(count, kv_heads, HEAD_SIZE)
    scores = (
        jnp.einsum(
            "tkgd,nkd->kgtn", heads_of_query, heads_of_key, preferred_element_type=jnp.float32
        )
        * scale
    )
    key_pos = (order[:, None] * tok_rows + jnp.arange(tok_rows, dtype=jnp.int32)[None, :]).reshape(-1)
    visible = (key_pos[None, :] <= positions[:, None]) & (
        doc_number(key_pos, bounds)[None, :] == query_doc[:, None]
    )
    masked = jnp.where(visible, scores, -1e30)
    best = jnp.max(masked, axis=-1)
    weights = jnp.where(visible, jnp.exp(masked - best[..., None]), 0.0)
    total = jnp.sum(weights, axis=-1)
    accum = jnp.einsum(
        "kgtn,nkd->kgtd",
        weights.astype(jnp.bfloat16),
        heads_of_value,
        preferred_element_type=jnp.float32,
    )
    attended = (
        (accum / total[..., None]).transpose(2, 0, 1, 3).reshape(tok_rows, -1).astype(jnp.bfloat16)
    )
    qwidth = attended.shape[1]
    proj_rows = lax.all_gather(out_weight, EXP, axis=0, tiled=True)
    feature_block = lax.all_to_all(
        attended.reshape(tok_rows, n_ctx, qwidth // n_ctx),
        CTX,
        split_axis=1,
        concat_axis=0,
        tiled=True,
    )
    feature_rows = jnp.take(
        feature_block.reshape(n_ctx, tok_rows, -1), order, axis=0
    ).reshape(n_ctx * tok_rows, -1)
    half = 8 * tok_rows
    attn_other = jnp.dot(feature_rows[half:], proj_rows, preferred_element_type=jnp.float32).astype(jnp.bfloat16)
    attn_own = jnp.dot(feature_rows[:half], proj_rows, preferred_element_type=jnp.float32).astype(jnp.bfloat16)
    attn_sum = rs_rel(attn_own, attn_other)
    hidden_state = resid[0].astype(jnp.float32) + attn_sum.astype(jnp.bfloat16).astype(jnp.float32)
    mean_square = jnp.mean(hidden_state * hidden_state, axis=-1, keepdims=True)
    normed = hidden_state * lax.rsqrt(mean_square + 1e-05) * norm_gain.astype(jnp.float32)
    normed_b = normed.astype(jnp.bfloat16)
    logits = jnp.dot(normed_b, router_weight, preferred_element_type=jnp.float32)
    n_experts = router_weight.shape[1]
    chosen = expert_ids[0, :, 0]
    picked = chosen[:, None] == jnp.arange(n_experts, dtype=jnp.int32)[None, :]
    score = jax.nn.sigmoid(jnp.sum(jnp.where(picked, logits, 0.0), axis=-1))
    routed = (normed * score[:, None]).astype(jnp.bfloat16)
    capacity = max(2, tok_rows // n_experts + tok_rows // (4 * n_experts))
    lower = jnp.tril(jnp.ones((tok_rows, tok_rows), jnp.float32), -1)
    earlier = jnp.dot(lower, picked.astype(jnp.float32), preferred_element_type=jnp.float32)
    slot_rank = jnp.sum(jnp.where(picked, earlier, 0.0), axis=-1).astype(jnp.int32)
    selector = picked[:, :, None] & (
        slot_rank[:, None, None] == jnp.arange(capacity, dtype=jnp.int32)[None, None, :]
    )
    selector_b = selector.astype(jnp.bfloat16)
    outgoing = jnp.einsum(
        "tes,td->esd", selector_b, routed, preferred_element_type=jnp.float32
    ).astype(jnp.bfloat16)
    arrived = lax.all_to_all(outgoing, EXP, split_axis=0, concat_axis=0, tiled=True)
    arrived_rows = arrived.reshape(-1, width)
    gate_local = gate_weight[0]
    up_local = up_weight[0]
    down_local = down_weight[0]
    piece = ag_rel(arrived_rows)
    rows_half = piece.shape[0] // 2

    def expert_rows(rows):
        gate = jnp.dot(rows, gate_local, preferred_element_type=jnp.float32)
        up = jnp.dot(rows, up_local, preferred_element_type=jnp.float32)
        inner = (jax.nn.silu(gate) * up).astype(jnp.bfloat16)
        return jnp.dot(inner, down_local, preferred_element_type=jnp.float32).astype(jnp.bfloat16)

    part_own = expert_rows(piece[:rows_half])
    part_other = expert_rows(piece[rows_half:])
    summed = rs_rel(part_own, part_other).astype(jnp.bfloat16)
    expert_out = summed.reshape(n_exp, capacity, width)
    returned = lax.all_to_all(expert_out, EXP, split_axis=0, concat_axis=0, tiled=True)
    combined = jnp.einsum("tes,esd->td", selector_b, returned, preferred_element_type=jnp.float32)
    layer_out = (hidden_state + combined).astype(jnp.bfloat16)
    return layer_out[None]


def solution(mesh):
    fine = Mesh(mesh.devices.reshape(4, 2, 2, 4, 4), CTX + EXP)
    in_specs = (
        P(EXP, CTX, None),
        P(EXP, CTX, None),
        P(EXP, CTX, None),
        P(EXP, None),
        P(EXP, CTX, None),
        P(CTX + EXP, None),
        P(),
        P(),
        P(EXP, CTX, None),
        P(EXP, None, CTX),
        P(EXP, None, CTX),
        P(EXP, CTX, None),
    )
    out_specs = P(EXP, CTX, None)
    return jax.shard_map(local, mesh=fine, in_specs=in_specs, out_specs=out_specs, check_vma=False)
```

```python
import math

import jax
import jax.numpy as jnp
from jax import lax
from jax.sharding import Mesh
from jax.sharding import PartitionSpec as P

HEAD_SIZE = 128
CTX = ("x", "zh", "core")
EXP = ("zl", "y")


def doc_number(positions, bounds):
    return jnp.sum((positions[:, None] >= bounds[None, :]).astype(jnp.int32), axis=1)


def _pp(v, axis, n, shift):
    return lax.ppermute(v, axis, [(i, (i + shift) % n) for i in range(n)])


def rel_index():
    x = lax.axis_index("x")
    zh = lax.axis_index("zh")
    c = lax.axis_index("core")
    dx = jnp.array([0, 0, -1, -1, 1, 1, -2, -2], jnp.int32)
    other_z = jnp.array([0, 1, 0, 1, 0, 1, 0, 1], jnp.int32)
    xs = (x + dx) % 4
    zs = (zh + other_z) % 2
    col = xs * 4 + zs * 2
    return jnp.concatenate([col + c, col + (1 - c)])


def ag_rel(b):
    h = b.shape[0] // 2
    zo = _pp(b, "zh", 2, 1)
    l1 = _pp(b, "x", 4, 1)
    r1 = _pp(b, "x", 4, -1)
    l2 = jnp.concatenate([_pp(l1[:h], "x", 4, 1), _pp(r1[h:], "x", 4, -1)], 0)
    l1o = _pp(zo, "x", 4, 1)
    r1o = _pp(zo, "x", 4, -1)
    r2o = jnp.concatenate([_pp(l1o[:h], "x", 4, 1), _pp(r1o[h:], "x", 4, -1)], 0)
    first = jnp.concatenate([b, zo, l1, l1o, r1, r1o], 0)
    last = jnp.concatenate([l2, r2o], 0)
    return jnp.concatenate([first, last, _pp(first, "core", 2, 1), _pp(last, "core", 2, 1)], 0)


def rs_rel(own, other):
    r = own.shape[0] // 8
    got = _pp(other, "core", 2, 1)
    blk = [own[i * r:(i + 1) * r].astype(jnp.float32) + got[i * r:(i + 1) * r].astype(jnp.float32) for i in range(8)]
    b = _pp(blk[7].astype(jnp.bfloat16), "x", 4, 1)
    c = _pp(blk[3].astype(jnp.bfloat16), "x", 4, -1)
    e = _pp((blk[5] + b.astype(jnp.float32)).astype(jnp.bfloat16), "x", 4, 1)
    a_src, _ = lax.optimization_barrier((blk[6].astype(jnp.bfloat16), c))
    a = _pp(a_src, "x", 4, -1)
    t1 = blk[1] + c.astype(jnp.float32) + e.astype(jnp.float32)
    z = _pp(t1.astype(jnp.bfloat16), "zh", 2, 1)
    d_src, _ = lax.optimization_barrier((blk[4].astype(jnp.bfloat16), e))
    d = _pp(d_src, "x", 4, 1)
    f = _pp((blk[2] + a.astype(jnp.float32)).astype(jnp.bfloat16), "x", 4, -1)
    t0 = blk[0] + f.astype(jnp.float32) + d.astype(jnp.float32)
    return t0 + z.astype(jnp.float32)


def local(
    queries,
    keys,
    values,
    doc_lengths,
    resid,
    out_weight,
    norm_gain,
    router_weight,
    expert_ids,
    gate_weight,
    up_weight,
    down_weight,
):
    tok_rows = queries.shape[1]
    width = resid.shape[2]
    n_ctx = 16
    n_exp = 16
    my_ctx = lax.axis_index("x") * 4 + lax.axis_index("zh") * 2 + lax.axis_index("core")
    positions = my_ctx * tok_rows + jnp.arange(tok_rows, dtype=jnp.int32)
    bounds = jnp.cumsum(doc_lengths[0])
    query_doc = doc_number(positions, bounds)
    kv_heads = keys.shape[2] // HEAD_SIZE
    kw = keys.shape[2]
    head_groups = queries.shape[2] // keys.shape[2]
    heads_of_query = queries[0].reshape(tok_rows, kv_heads, head_groups, HEAD_SIZE)
    scale = 1.0 / math.sqrt(HEAD_SIZE)
    order = rel_index()
    kv_piece = ag_rel(jnp.concatenate([keys[0], values[0]], axis=1))
    key_piece = kv_piece[:, :kw]
    value_piece = kv_piece[:, kw:]
    count = key_piece.shape[0]
    heads_of_key = key_piece.reshape(count, kv_heads, HEAD_SIZE)
    heads_of_value = value_piece.reshape(count, kv_heads, HEAD_SIZE)
    scores = (
        jnp.einsum(
            "tkgd,nkd->kgtn", heads_of_query, heads_of_key, preferred_element_type=jnp.float32
        )
        * scale
    )
    key_pos = (order[:, None] * tok_rows + jnp.arange(tok_rows, dtype=jnp.int32)[None, :]).reshape(-1)
    visible = (key_pos[None, :] <= positions[:, None]) & (
        doc_number(key_pos, bounds)[None, :] == query_doc[:, None]
    )
    masked = jnp.where(visible, scores, -1e30)
    best = jnp.max(masked, axis=-1)
    weights = jnp.where(visible, jnp.exp(masked - best[..., None]), 0.0)
    total = jnp.sum(weights, axis=-1)
    accum = jnp.einsum(
        "kgtn,nkd->kgtd",
        weights.astype(jnp.bfloat16),
        heads_of_value,
        preferred_element_type=jnp.float32,
    )
    attended = (
        (accum / total[..., None]).transpose(2, 0, 1, 3).reshape(tok_rows, -1).astype(jnp.bfloat16)
    )
    qwidth = attended.shape[1]
    proj_rows = lax.all_gather(out_weight, EXP, axis=0, tiled=True)
    feature_block = lax.all_to_all(
        attended.reshape(tok_rows, n_ctx, qwidth // n_ctx),
        CTX,
        split_axis=1,
        concat_axis=0,
        tiled=True,
    )
    feature_rows = jnp.take(
        feature_block.reshape(n_ctx, tok_rows, -1), order, axis=0
    ).reshape(n_ctx * tok_rows, -1)
    half = 8 * tok_rows
    attn_other = jnp.dot(feature_rows[half:], proj_rows, preferred_element_type=jnp.float32).astype(jnp.bfloat16)
    attn_own = jnp.dot(feature_rows[:half], proj_rows, preferred_element_type=jnp.float32).astype(jnp.bfloat16)
    attn_sum = rs_rel(attn_own, attn_other)
    hidden_state = resid[0].astype(jnp.float32) + attn_sum.astype(jnp.bfloat16).astype(jnp.float32)
    mean_square = jnp.mean(hidden_state * hidden_state, axis=-1, keepdims=True)
    normed = hidden_state * lax.rsqrt(mean_square + 1e-05) * norm_gain.astype(jnp.float32)
    normed_b = normed.astype(jnp.bfloat16)
    logits = jnp.dot(normed_b, router_weight, preferred_element_type=jnp.float32)
    n_experts = router_weight.shape[1]
    chosen = expert_ids[0, :, 0]
    picked = chosen[:, None] == jnp.arange(n_experts, dtype=jnp.int32)[None, :]
    score = jax.nn.sigmoid(jnp.sum(jnp.where(picked, logits, 0.0), axis=-1))
    routed = (normed * score[:, None]).astype(jnp.bfloat16)
    capacity = max(2, tok_rows // n_experts + tok_rows // (4 * n_experts))
    lower = jnp.tril(jnp.ones((tok_rows, tok_rows), jnp.float32), -1)
    earlier = jnp.dot(lower, picked.astype(jnp.float32), preferred_element_type=jnp.float32)
    slot_rank = jnp.sum(jnp.where(picked, earlier, 0.0), axis=-1).astype(jnp.int32)
    selector = picked[:, :, None] & (
        slot_rank[:, None, None] == jnp.arange(capacity, dtype=jnp.int32)[None, None, :]
    )
    selector_b = selector.astype(jnp.bfloat16)
    outgoing = jnp.einsum(
        "tes,td->esd", selector_b, routed, preferred_element_type=jnp.float32
    ).astype(jnp.bfloat16)
    arrived = lax.all_to_all(outgoing, EXP, split_axis=0, concat_axis=0, tiled=True)
    arrived_rows = arrived.reshape(-1, width)
    gate_local = gate_weight[0]
    up_local = up_weight[0]
    down_local = down_weight[0]
    piece = ag_rel(arrived_rows)
    rows_half = piece.shape[0] // 2

    def expert_rows(rows):
        gate = jnp.dot(rows, gate_local, preferred_element_type=jnp.float32)
        up = jnp.dot(rows, up_local, preferred_element_type=jnp.float32)
        inner = (jax.nn.silu(gate) * up).astype(jnp.bfloat16)
        return jnp.dot(inner, down_local, preferred_element_type=jnp.float32).astype(jnp.bfloat16)

    part_own = expert_rows(piece[:rows_half])
    part_other = expert_rows(piece[rows_half:])
    summed = rs_rel(part_own, part_other).astype(jnp.bfloat16)
    expert_out = summed.reshape(n_exp, capacity, width)
    returned = lax.all_to_all(expert_out, EXP, split_axis=0, concat_axis=0, tiled=True)
    combined = jnp.einsum("tes,esd->td", selector_b, returned, preferred_element_type=jnp.float32)
    layer_out = (hidden_state + combined).astype(jnp.bfloat16)
    return layer_out[None]


def solution(mesh):
    fine = Mesh(mesh.devices.reshape(4, 2, 2, 4, 4), CTX + EXP)
    in_specs = (
        P(EXP, CTX, None),
        P(EXP, CTX, None),
        P(EXP, CTX, None),
        P(EXP, None),
        P(EXP, CTX, None),
        P(CTX + EXP, None),
        P(),
        P(),
        P(EXP, CTX, None),
        P(EXP, None, CTX),
        P(EXP, None, CTX),
        P(EXP, CTX, None),
    )
    out_specs = P(EXP, CTX, None)
    return jax.shard_map(local, mesh=fine, in_specs=in_specs, out_specs=out_specs, check_vma=False)
```

```python
import math

import jax
import jax.numpy as jnp
from jax import lax
from jax.sharding import Mesh
from jax.sharding import PartitionSpec as P

HEAD_SIZE = 128
CTX = ("x", "zh", "core")
EXP = ("zl", "y")


def doc_number(positions, bounds):
    return jnp.sum((positions[:, None] >= bounds[None, :]).astype(jnp.int32), axis=1)


def _pp(v, axis, n, shift):
    return lax.ppermute(v, axis, [(i, (i + shift) % n) for i in range(n)])


def rel_index():
    x = lax.axis_index("x")
    zh = lax.axis_index("zh")
    c = lax.axis_index("core")
    dx = jnp.array([0, 0, -1, -1, 1, 1, -2, -2], jnp.int32)
    other_z = jnp.array([0, 1, 0, 1, 0, 1, 0, 1], jnp.int32)
    xs = (x + dx) % 4
    zs = (zh + other_z) % 2
    col = xs * 4 + zs * 2
    return jnp.concatenate([col + c, col + (1 - c)])


def ag_rel(b):
    zo = _pp(b, "zh", 2, 1)
    l1 = _pp(b, "x", 4, 1)
    r1 = _pp(b, "x", 4, -1)
    l1o = _pp(zo, "x", 4, 1)
    r1o = _pp(zo, "x", 4, -1)
    l2 = _pp(l1, "x", 4, 1)
    r2o = _pp(r1o, "x", 4, -1)
    first = jnp.concatenate([b, zo, l1, l1o, r1, r1o], 0)
    last = jnp.concatenate([l2, r2o], 0)
    return jnp.concatenate([first, last, _pp(first, "core", 2, 1), _pp(last, "core", 2, 1)], 0)


def rs_rel(own, other):
    r = own.shape[0] // 8
    early, late = (7, 3, 5), (6, 4, 2, 1, 0)
    got_early = _pp(jnp.concatenate([other[i * r:(i + 1) * r] for i in early], 0), "core", 2, 1)
    got_late = _pp(jnp.concatenate([other[i * r:(i + 1) * r] for i in late], 0), "core", 2, 1)
    got = {i: got_early[k * r:(k + 1) * r] for k, i in enumerate(early)}
    got.update({i: got_late[k * r:(k + 1) * r] for k, i in enumerate(late)})
    blk = [own[i * r:(i + 1) * r].astype(jnp.float32) + got[i].astype(jnp.float32) for i in range(8)]
    b = _pp(blk[7].astype(jnp.bfloat16), "x", 4, 1)
    c = _pp(blk[3].astype(jnp.bfloat16), "x", 4, -1)
    e = _pp((blk[5] + b.astype(jnp.float32)).astype(jnp.bfloat16), "x", 4, 1)
    a_src, _ = lax.optimization_barrier((blk[6].astype(jnp.bfloat16), c))
    a = _pp(a_src, "x", 4, -1)
    t1 = blk[1] + c.astype(jnp.float32) + e.astype(jnp.float32)
    z = _pp(t1.astype(jnp.bfloat16), "zh", 2, 1)
    d_src, _ = lax.optimization_barrier((blk[4].astype(jnp.bfloat16), e))
    d = _pp(d_src, "x", 4, 1)
    f = _pp((blk[2] + a.astype(jnp.float32)).astype(jnp.bfloat16), "x", 4, -1)
    t0 = blk[0] + f.astype(jnp.float32) + d.astype(jnp.float32)
    return t0 + z.astype(jnp.float32)


def local(
    queries,
    keys,
    values,
    doc_lengths,
    resid,
    out_weight,
    norm_gain,
    router_weight,
    expert_ids,
    gate_weight,
    up_weight,
    down_weight,
):
    tok_rows = queries.shape[1]
    width = resid.shape[2]
    n_ctx = 16
    n_exp = 16
    my_ctx = lax.axis_index("x") * 4 + lax.axis_index("zh") * 2 + lax.axis_index("core")
    positions = my_ctx * tok_rows + jnp.arange(tok_rows, dtype=jnp.int32)
    bounds = jnp.cumsum(doc_lengths[0])
    query_doc = doc_number(positions, bounds)
    kv_heads = keys.shape[2] // HEAD_SIZE
    kw = keys.shape[2]
    head_groups = queries.shape[2] // keys.shape[2]
    heads_of_query = queries[0].reshape(tok_rows, kv_heads, head_groups, HEAD_SIZE)
    scale = 1.0 / math.sqrt(HEAD_SIZE)
    order = rel_index()
    kv_piece = ag_rel(jnp.concatenate([keys[0], values[0]], axis=1))
    key_piece = kv_piece[:, :kw]
    value_piece = kv_piece[:, kw:]
    count = key_piece.shape[0]
    heads_of_key = key_piece.reshape(count, kv_heads, HEAD_SIZE)
    heads_of_value = value_piece.reshape(count, kv_heads, HEAD_SIZE)
    scores = (
        jnp.einsum(
            "tkgd,nkd->kgtn", heads_of_query, heads_of_key, preferred_element_type=jnp.float32
        )
        * scale
    )
    key_pos = (order[:, None] * tok_rows + jnp.arange(tok_rows, dtype=jnp.int32)[None, :]).reshape(-1)
    visible = (key_pos[None, :] <= positions[:, None]) & (
        doc_number(key_pos, bounds)[None, :] == query_doc[:, None]
    )
    masked = jnp.where(visible, scores, -1e30)
    best = jnp.max(masked, axis=-1)
    weights = jnp.where(visible, jnp.exp(masked - best[..., None]), 0.0)
    total = jnp.sum(weights, axis=-1)
    accum = jnp.einsum(
        "kgtn,nkd->kgtd",
        weights.astype(jnp.bfloat16),
        heads_of_value,
        preferred_element_type=jnp.float32,
    )
    attended = (
        (accum / total[..., None]).transpose(2, 0, 1, 3).reshape(tok_rows, -1).astype(jnp.bfloat16)
    )
    qwidth = attended.shape[1]
    proj_rows = lax.all_gather(out_weight, EXP, axis=0, tiled=True)
    feature_block = lax.all_to_all(
        attended.reshape(tok_rows, n_ctx, qwidth // n_ctx),
        CTX,
        split_axis=1,
        concat_axis=0,
        tiled=True,
    )
    feature_rows = jnp.take(
        feature_block.reshape(n_ctx, tok_rows, -1), order, axis=0
    ).reshape(n_ctx * tok_rows, -1)
    half = 8 * tok_rows
    attn_other = jnp.dot(feature_rows[half:], proj_rows, preferred_element_type=jnp.float32).astype(jnp.bfloat16)
    attn_own = jnp.dot(feature_rows[:half], proj_rows, preferred_element_type=jnp.float32).astype(jnp.bfloat16)
    attn_sum = rs_rel(attn_own, attn_other)
    hidden_state = resid[0].astype(jnp.float32) + attn_sum.astype(jnp.bfloat16).astype(jnp.float32)
    mean_square = jnp.mean(hidden_state * hidden_state, axis=-1, keepdims=True)
    normed = hidden_state * lax.rsqrt(mean_square + 1e-05) * norm_gain.astype(jnp.float32)
    normed_b = normed.astype(jnp.bfloat16)
    logits = jnp.dot(normed_b, router_weight, preferred_element_type=jnp.float32)
    n_experts = router_weight.shape[1]
    chosen = expert_ids[0, :, 0]
    picked = chosen[:, None] == jnp.arange(n_experts, dtype=jnp.int32)[None, :]
    score = jax.nn.sigmoid(jnp.sum(jnp.where(picked, logits, 0.0), axis=-1))
    routed = (normed * score[:, None]).astype(jnp.bfloat16)
    capacity = max(2, tok_rows // n_experts + tok_rows // (4 * n_experts))
    lower = jnp.tril(jnp.ones((tok_rows, tok_rows), jnp.float32), -1)
    earlier = jnp.dot(lower, picked.astype(jnp.float32), preferred_element_type=jnp.float32)
    slot_rank = jnp.sum(jnp.where(picked, earlier, 0.0), axis=-1).astype(jnp.int32)
    selector = picked[:, :, None] & (
        slot_rank[:, None, None] == jnp.arange(capacity, dtype=jnp.int32)[None, None, :]
    )
    selector_b = selector.astype(jnp.bfloat16)
    outgoing = jnp.einsum(
        "tes,td->esd", selector_b, routed, preferred_element_type=jnp.float32
    ).astype(jnp.bfloat16)
    arrived = lax.all_to_all(outgoing, EXP, split_axis=0, concat_axis=0, tiled=True)
    arrived_rows = arrived.reshape(-1, width)
    gate_local = gate_weight[0]
    up_local = up_weight[0]
    down_local = down_weight[0]
    piece = ag_rel(arrived_rows)
    rows_half = piece.shape[0] // 2

    def expert_rows(rows):
        gate = jnp.dot(rows, gate_local, preferred_element_type=jnp.float32)
        up = jnp.dot(rows, up_local, preferred_element_type=jnp.float32)
        inner = (jax.nn.silu(gate) * up).astype(jnp.bfloat16)
        return jnp.dot(inner, down_local, preferred_element_type=jnp.float32).astype(jnp.bfloat16)

    part_own = expert_rows(piece[:rows_half])
    part_other = expert_rows(piece[rows_half:])
    summed = rs_rel(part_own, part_other).astype(jnp.bfloat16)
    expert_out = summed.reshape(n_exp, capacity, width)
    returned = lax.all_to_all(expert_out, EXP, split_axis=0, concat_axis=0, tiled=True)
    combined = jnp.einsum("tes,esd->td", selector_b, returned, preferred_element_type=jnp.float32)
    layer_out = (hidden_state + combined).astype(jnp.bfloat16)
    return layer_out[None]


def solution(mesh):
    fine = Mesh(mesh.devices.reshape(4, 2, 2, 4, 4), CTX + EXP)
    in_specs = (
        P(EXP, CTX, None),
        P(EXP, CTX, None),
        P(EXP, CTX, None),
        P(EXP, None),
        P(EXP, CTX, None),
        P(CTX + EXP, None),
        P(),
        P(),
        P(EXP, CTX, None),
        P(EXP, None, CTX),
        P(EXP, None, CTX),
        P(EXP, CTX, None),
    )
    out_specs = P(EXP, CTX, None)
    return jax.shard_map(local, mesh=fine, in_specs=in_specs, out_specs=out_specs, check_vma=False)
```

```python
import math

import jax
import jax.numpy as jnp
from jax import lax
from jax.sharding import Mesh
from jax.sharding import PartitionSpec as P

HEAD_SIZE = 128
CTX = ("x", "zh", "core")
EXP = ("zl", "y")


def doc_number(positions, bounds):
    return jnp.sum((positions[:, None] >= bounds[None, :]).astype(jnp.int32), axis=1)


def _pp(v, axis, n, shift):
    return lax.ppermute(v, axis, [(i, (i + shift) % n) for i in range(n)])


def rel_index():
    x = lax.axis_index("x")
    zh = lax.axis_index("zh")
    c = lax.axis_index("core")
    dx = jnp.array([0, 0, -1, -1, 1, 1, -2, -2], jnp.int32)
    other_z = jnp.array([0, 1, 0, 1, 0, 1, 0, 1], jnp.int32)
    xs = (x + dx) % 4
    zs = (zh + other_z) % 2
    col = xs * 4 + zs * 2
    return jnp.concatenate([col + c, col + (1 - c)])


def ag_rel(b):
    zo = _pp(b, "zh", 2, 1)
    l1 = _pp(b, "x", 4, 1)
    r1 = _pp(b, "x", 4, -1)
    l1o = _pp(zo, "x", 4, 1)
    r1o = _pp(zo, "x", 4, -1)
    l2_src, _ = lax.optimization_barrier((l1, l1o))
    l2 = _pp(l2_src, "x", 4, 1)
    r2o = _pp(r1o, "x", 4, -1)
    first = jnp.concatenate([b, zo, l1, l1o, r1, r1o], 0)
    last = jnp.concatenate([l2, r2o], 0)
    return jnp.concatenate([first, last, _pp(first, "core", 2, 1), _pp(last, "core", 2, 1)], 0)


def rs_rel(own, other):
    r = own.shape[0] // 8
    got = _pp(other, "core", 2, 1)
    blk = [own[i * r:(i + 1) * r].astype(jnp.float32) + got[i * r:(i + 1) * r].astype(jnp.float32) for i in range(8)]
    b = _pp(blk[7].astype(jnp.bfloat16), "x", 4, 1)
    c = _pp(blk[3].astype(jnp.bfloat16), "x", 4, -1)
    e = _pp((blk[5] + b.astype(jnp.float32)).astype(jnp.bfloat16), "x", 4, 1)
    a_src, _ = lax.optimization_barrier((blk[6].astype(jnp.bfloat16), c))
    a = _pp(a_src, "x", 4, -1)
    t1 = blk[1] + c.astype(jnp.float32) + e.astype(jnp.float32)
    z = _pp(t1.astype(jnp.bfloat16), "zh", 2, 1)
    d_src, _ = lax.optimization_barrier((blk[4].astype(jnp.bfloat16), e))
    d = _pp(d_src, "x", 4, 1)
    f = _pp((blk[2] + a.astype(jnp.float32)).astype(jnp.bfloat16), "x", 4, -1)
    t0 = blk[0] + f.astype(jnp.float32) + d.astype(jnp.float32)
    return t0 + z.astype(jnp.float32)


def local(
    queries,
    keys,
    values,
    doc_lengths,
    resid,
    out_weight,
    norm_gain,
    router_weight,
    expert_ids,
    gate_weight,
    up_weight,
    down_weight,
):
    tok_rows = queries.shape[1]
    width = resid.shape[2]
    n_ctx = 16
    n_exp = 16
    my_ctx = lax.axis_index("x") * 4 + lax.axis_index("zh") * 2 + lax.axis_index("core")
    positions = my_ctx * tok_rows + jnp.arange(tok_rows, dtype=jnp.int32)
    bounds = jnp.cumsum(doc_lengths[0])
    query_doc = doc_number(positions, bounds)
    kv_heads = keys.shape[2] // HEAD_SIZE
    kw = keys.shape[2]
    head_groups = queries.shape[2] // keys.shape[2]
    heads_of_query = queries[0].reshape(tok_rows, kv_heads, head_groups, HEAD_SIZE)
    scale = 1.0 / math.sqrt(HEAD_SIZE)
    order = rel_index()
    kv_piece = ag_rel(jnp.concatenate([keys[0], values[0]], axis=1))
    key_piece = kv_piece[:, :kw]
    value_piece = kv_piece[:, kw:]
    count = key_piece.shape[0]
    heads_of_key = key_piece.reshape(count, kv_heads, HEAD_SIZE)
    heads_of_value = value_piece.reshape(count, kv_heads, HEAD_SIZE)
    scores = (
        jnp.einsum(
            "tkgd,nkd->kgtn", heads_of_query, heads_of_key, preferred_element_type=jnp.float32
        )
        * scale
    )
    key_pos = (order[:, None] * tok_rows + jnp.arange(tok_rows, dtype=jnp.int32)[None, :]).reshape(-1)
    visible = (key_pos[None, :] <= positions[:, None]) & (
        doc_number(key_pos, bounds)[None, :] == query_doc[:, None]
    )
    masked = jnp.where(visible, scores, -1e30)
    best = jnp.max(masked, axis=-1)
    weights = jnp.where(visible, jnp.exp(masked - best[..., None]), 0.0)
    total = jnp.sum(weights, axis=-1)
    accum = jnp.einsum(
        "kgtn,nkd->kgtd",
        weights.astype(jnp.bfloat16),
        heads_of_value,
        preferred_element_type=jnp.float32,
    )
    attended = (
        (accum / total[..., None]).transpose(2, 0, 1, 3).reshape(tok_rows, -1).astype(jnp.bfloat16)
    )
    qwidth = attended.shape[1]
    proj_rows = lax.all_gather(out_weight, EXP, axis=0, tiled=True)
    feature_block = lax.all_to_all(
        attended.reshape(tok_rows, n_ctx, qwidth // n_ctx),
        CTX,
        split_axis=1,
        concat_axis=0,
        tiled=True,
    )
    feature_rows = jnp.take(
        feature_block.reshape(n_ctx, tok_rows, -1), order, axis=0
    ).reshape(n_ctx * tok_rows, -1)
    half = 8 * tok_rows
    attn_other = jnp.dot(feature_rows[half:], proj_rows, preferred_element_type=jnp.float32).astype(jnp.bfloat16)
    attn_own = jnp.dot(feature_rows[:half], proj_rows, preferred_element_type=jnp.float32).astype(jnp.bfloat16)
    attn_sum = rs_rel(attn_own, attn_other)
    hidden_state = resid[0].astype(jnp.float32) + attn_sum.astype(jnp.bfloat16).astype(jnp.float32)
    mean_square = jnp.mean(hidden_state * hidden_state, axis=-1, keepdims=True)
    normed = hidden_state * lax.rsqrt(mean_square + 1e-05) * norm_gain.astype(jnp.float32)
    normed_b = normed.astype(jnp.bfloat16)
    logits = jnp.dot(normed_b, router_weight, preferred_element_type=jnp.float32)
    n_experts = router_weight.shape[1]
    chosen = expert_ids[0, :, 0]
    picked = chosen[:, None] == jnp.arange(n_experts, dtype=jnp.int32)[None, :]
    score = jax.nn.sigmoid(jnp.sum(jnp.where(picked, logits, 0.0), axis=-1))
    routed = (normed * score[:, None]).astype(jnp.bfloat16)
    capacity = max(2, tok_rows // n_experts + tok_rows // (4 * n_experts))
    lower = jnp.tril(jnp.ones((tok_rows, tok_rows), jnp.float32), -1)
    earlier = jnp.dot(lower, picked.astype(jnp.float32), preferred_element_type=jnp.float32)
    slot_rank = jnp.sum(jnp.where(picked, earlier, 0.0), axis=-1).astype(jnp.int32)
    selector = picked[:, :, None] & (
        slot_rank[:, None, None] == jnp.arange(capacity, dtype=jnp.int32)[None, None, :]
    )
    selector_b = selector.astype(jnp.bfloat16)
    outgoing = jnp.einsum(
        "tes,td->esd", selector_b, routed, preferred_element_type=jnp.float32
    ).astype(jnp.bfloat16)
    arrived = lax.all_to_all(outgoing, EXP, split_axis=0, concat_axis=0, tiled=True)
    arrived_rows = arrived.reshape(-1, width)
    gate_local = gate_weight[0]
    up_local = up_weight[0]
    down_local = down_weight[0]
    piece = ag_rel(arrived_rows)
    rows_half = piece.shape[0] // 2

    def expert_rows(rows):
        gate = jnp.dot(rows, gate_local, preferred_element_type=jnp.float32)
        up = jnp.dot(rows, up_local, preferred_element_type=jnp.float32)
        inner = (jax.nn.silu(gate) * up).astype(jnp.bfloat16)
        return jnp.dot(inner, down_local, preferred_element_type=jnp.float32).astype(jnp.bfloat16)

    part_own = expert_rows(piece[:rows_half])
    part_other = expert_rows(piece[rows_half:])
    summed = rs_rel(part_own, part_other).astype(jnp.bfloat16)
    expert_out = summed.reshape(n_exp, capacity, width)
    returned = lax.all_to_all(expert_out, EXP, split_axis=0, concat_axis=0, tiled=True)
    combined = jnp.einsum("tes,esd->td", selector_b, returned, preferred_element_type=jnp.float32)
    layer_out = (hidden_state + combined).astype(jnp.bfloat16)
    return layer_out[None]


def solution(mesh):
    fine = Mesh(mesh.devices.reshape(4, 2, 2, 4, 4), CTX + EXP)
    in_specs = (
        P(EXP, CTX, None),
        P(EXP, CTX, None),
        P(EXP, CTX, None),
        P(EXP, None),
        P(EXP, CTX, None),
        P(CTX + EXP, None),
        P(),
        P(),
        P(EXP, CTX, None),
        P(EXP, None, CTX),
        P(EXP, None, CTX),
        P(EXP, CTX, None),
    )
    out_specs = P(EXP, CTX, None)
    return jax.shard_map(local, mesh=fine, in_specs=in_specs, out_specs=out_specs, check_vma=False)
```
